768 devices in a mesh: fsdp: 48 (over z, x_lo, core), seq: 16 (over x_hi, y).
Axes of the slice: x: 4 (x_hi: 2, x_lo: 2; x = x_hi * 2 + x_lo), y: 8, z: 12, core: 2. Of those that a mesh axis runs over, the one named last changes fastest.
Arguments:
- tokens: bfloat16 [48, 2048, 2880], P('fsdp', 'seq'), may hold values from -6 to 6
- queries: bfloat16 [48, 2048, 2048], P('fsdp', 'seq'), may hold values from -6 to 6
- kv_weight: bfloat16 [2880, 512], P('fsdp'), may hold values from -0.109375 to 0.109375
- sink_logit_values: float32 [32], replicated, may hold values from 1 to 6
- roll_offsets: int32 [48], P('fsdp'), may hold values from 0 to 2047
- out_grad: bfloat16 [48, 2048, 2048], P('fsdp', 'seq'), may hold values from -6 to 6
Outputs:
- attn_out: bfloat16 [48, 2048, 2048], P('fsdp', 'seq')
- query_grad: bfloat16 [48, 2048, 2048], P('fsdp', 'seq')
- token_grad: bfloat16 [48, 2048, 2880], P('fsdp', 'seq')
- weight_grad: float32 [16, 720, 128], P('seq', 'fsdp')
The draws below stay inside these ranges and needn't reach their ends.
All inputs are finite; a program needn't handle non-finite values.
Results may differ from the reference program's by a relative error of at most 0.012.
Values may be sent and summed in bfloat16 or wider, within the bound.
No kernel may reach another device: no remote copies, remote signals or barrier semaphores. Data moves between devices by JAX's collectives and lax.ppermute only.
A program may use at most 32 MiB of HBM per device.

```python
import jax
import jax.numpy as jnp
from jax import lax

D = 2880
QUERY_HEADS = 32
KEY_VALUE_HEADS = 4
HEAD_SIZE = 64
WINDOW = 128
STREAMS = 48
SEQLEN = 2048
QW = 2048
KW = 512
GRAD_BLOCK_ROWS = 720
N_SEQ = 16


def with_ends(array, key, least, high):
    longest = array.shape.index(max(array.shape))
    spots = []
    for shift in (0, 1):
        where = [jax.random.randint(jax.random.fold_in(key, axis), (), 0, length) for axis, length in enumerate(array.shape)]
        where[longest] = (where[longest] + shift) % array.shape[longest]
        spots.append(tuple(where))
    return array.at[spots[0]].set(least).at[spots[1]].set(high)


def with_spikes(entries, stream_key, source, target, shards_of, factor):
    def block_of(dim):
        return (jnp.arange(entries.shape[dim]) // (entries.shape[dim] // shards_of)).reshape((-1,) + (1,) * (entries.ndim - 1 - dim))

    one_side = jax.random.permutation(stream_key, shards_of)[block_of(target)]
    far = (block_of(target) + shards_of // 2) % shards_of
    return jnp.where((block_of(source) == one_side) | (block_of(source) == far), factor * entries, entries)


def block_scale(own_key, dims, split, low, top_value):
    def one(axis_at, blocks):
        draws = jax.random.uniform(jax.random.fold_in(jax.random.fold_in(own_key, 6), axis_at), (blocks,), jnp.float32, low / len(split), top_value / len(split))
        return jnp.repeat(jnp.exp(draws), dims[axis_at] // blocks).reshape((-1,) + (1,) * (len(dims) - axis_at - 1))

    loudness = one(*split[0])
    for cut in split[1:]:
        loudness = loudness * one(*cut)
    return loudness


def bell_draw(key, shape, deviation, reach, pieces=(), kind=jnp.bfloat16):
    gain = block_scale(key, shape, pieces, -0.22, 0.18) if pieces else 1.0
    drawn = jax.random.normal(key, shape, jnp.float32) * deviation * gain
    return jnp.minimum(jnp.maximum(drawn, -reach), reach).astype(kind)


def noise_with(rng, dims, width, bound, shards, heavy, kind=jnp.bfloat16):
    entries = width * jax.random.normal(rng, dims, jnp.float32)
    if shards:
        entries = entries * block_scale(rng, dims, shards, -0.22, 0.18)
    return jnp.clip(with_spikes(entries, jax.random.fold_in(rng, 3), *heavy), -bound, bound).astype(kind)


def setup_inputs(seed: int = 0) -> dict:
    seeds = jax.random.split(jax.random.key(seed), 7)
    return {
        "tokens": noise_with(seeds[0], (STREAMS, SEQLEN, D), 1.0, 6.0, ((0, 48), (1, 16)), (0, 2, 48, 3.25)),
        "queries": bell_draw(seeds[1], (STREAMS, SEQLEN, QW), 1.0, 6.0, ((0, 48), (1, 16))),
        "kv_weight": bell_draw(seeds[2], (D, KW), D ** -0.5, 0.109375, ((0, 48),)),
        "sink_logit_values": jnp.clip(jax.random.uniform(seeds[3], (QUERY_HEADS,), jnp.float32, 1.0, 6.0), 1.0, 6.0),
        "roll_offsets": with_ends(jax.random.randint(seeds[4], (STREAMS,), 0, SEQLEN), jax.random.fold_in(seeds[4], 1), 0, SEQLEN - 1).astype(jnp.int32),
        "out_grad": noise_with(seeds[5], (STREAMS, SEQLEN, QW), 1.0, 6.0, ((0, 48), (1, 16)), (1, 2, 16, 2.0)),
    }


rope_base = 150000.0


def rope_tables(positions):
    half_width = HEAD_SIZE // 2
    frequency = rope_base ** (-jnp.arange(half_width, dtype=jnp.float32) / half_width)
    angle = positions.astype(jnp.float32)[:, None] * frequency[None, :]
    return jnp.cos(angle), jnp.sin(angle)


def apply_rotary(values, cosine_lookup, sine_lookup, head_count, direction):
    row_count = values.shape[0]
    halves = values.reshape(row_count, head_count, 2, HEAD_SIZE // 2)
    front_half = halves[:, :, 0]
    back_half = halves[:, :, 1]
    cosine_rows = cosine_lookup[:, None, :]
    sine_rows = sine_lookup[:, None, :] * direction
    turned = jnp.stack([front_half * cosine_rows - back_half * sine_rows,
                        front_half * sine_rows + back_half * cosine_rows], axis=2)
    return turned.reshape(row_count, head_count * HEAD_SIZE)


def attend_group(query_g, key_g, value_g, grad_g, sink_g, allowed):
    score_scale = HEAD_SIZE ** -0.5
    query_f = query_g.astype(jnp.float32)
    key_f = key_g.astype(jnp.float32)
    value_f = value_g.astype(jnp.float32)
    grad_f = grad_g.astype(jnp.float32)
    scores = jnp.einsum('bgd,kd->gbk', query_f, key_f) * score_scale
    exponent = jnp.where(allowed[None], jnp.exp(scores), 0.0)
    denominator = jnp.exp(sink_g)[:, None] + jnp.sum(exponent, axis=2)
    softmax_w = exponent / denominator[:, :, None]
    softmax_b = softmax_w.astype(jnp.bfloat16).astype(jnp.float32)
    attended = jnp.einsum('gbk,kd->bgd', softmax_b, value_f)
    dprob = jnp.einsum('bgd,kd->gbk', grad_f, value_f)
    row_delta = jnp.sum(softmax_w * dprob, axis=2)
    dscore = (softmax_w * (dprob - row_delta[:, :, None]) * score_scale).astype(jnp.bfloat16).astype(jnp.float32)
    query_diff = jnp.einsum('gbk,kd->bgd', dscore, key_f)
    key_diff = jnp.einsum('gbk,bgd->kd', dscore, query_f)
    value_diff = jnp.einsum('gbk,bgd->kd', softmax_b, grad_f)
    return attended.astype(jnp.bfloat16), query_diff, key_diff, value_diff


def attend_block(query_block, key_block, gradient_block, sink_logit_values, key_first):
    block_row_span = query_block.shape[0]
    key_row_slice = key_block.shape[0]
    group_width = QUERY_HEADS // KEY_VALUE_HEADS
    key_span_width = KEY_VALUE_HEADS * HEAD_SIZE
    rows_idx = jnp.arange(block_row_span, dtype=jnp.int32)[:, None]
    cols_idx = jnp.arange(key_row_slice, dtype=jnp.int32)[None, :]
    allowed = (cols_idx > rows_idx) & (cols_idx <= rows_idx + WINDOW) & (cols_idx + key_first >= 0)
    query_head_rows = query_block.reshape(block_row_span, KEY_VALUE_HEADS, group_width, HEAD_SIZE).transpose(1, 0, 2, 3)
    gradient_heads = gradient_block.reshape(block_row_span, KEY_VALUE_HEADS, group_width, HEAD_SIZE).transpose(1, 0, 2, 3)
    key_head_rows = key_block[:, :key_span_width].reshape(key_row_slice, KEY_VALUE_HEADS, HEAD_SIZE).transpose(1, 0, 2)
    value_head_rows = key_block[:, key_span_width:].reshape(key_row_slice, KEY_VALUE_HEADS, HEAD_SIZE).transpose(1, 0, 2)
    sink_per_head = sink_logit_values.reshape(KEY_VALUE_HEADS, group_width)

    def per_group(packed):
        return attend_group(packed[0], packed[1], packed[2], packed[3], packed[4], allowed)

    attended, query_diff, key_diff, value_diff = lax.map(per_group, (query_head_rows, key_head_rows, value_head_rows, gradient_heads, sink_per_head))
    attended = attended.transpose(1, 0, 2, 3).reshape(block_row_span, QUERY_HEADS * HEAD_SIZE)
    query_diff = query_diff.transpose(1, 0, 2, 3).reshape(block_row_span, QUERY_HEADS * HEAD_SIZE)
    kv_diff = jnp.concatenate([key_diff.transpose(1, 0, 2).reshape(key_row_slice, key_span_width),
                               value_diff.transpose(1, 0, 2).reshape(key_row_slice, key_span_width)], axis=1)
    return attended, query_diff, kv_diff


def band_pass(query_rot, keys_all, grad_out, sink_logit_values, row_start):
    row_total = query_rot.shape[0]
    block_row_span = min(row_total, 512)

    def block_step(grad_all, block_index):
        block_begin = block_index * block_row_span
        query_block = lax.dynamic_slice_in_dim(query_rot, block_begin, block_row_span, 0)
        key_block = lax.dynamic_slice_in_dim(keys_all, block_begin, block_row_span + WINDOW, 0)
        gradient_block = lax.dynamic_slice_in_dim(grad_out, block_begin, block_row_span, 0)
        attended, query_diff, kv_diff = attend_block(query_block, key_block, gradient_block, sink_logit_values, row_start + block_begin - WINDOW)
        previous = lax.dynamic_slice_in_dim(grad_all, block_begin, block_row_span + WINDOW, 0)
        grad_all = lax.dynamic_update_slice_in_dim(grad_all, previous + kv_diff, block_begin, 0)
        return grad_all, (attended, query_diff)

    start_grad = jnp.zeros((row_total + WINDOW, keys_all.shape[1]), jnp.float32)
    grad_all, (attended, query_diff) = lax.scan(block_step, start_grad, jnp.arange(row_total // block_row_span, dtype=jnp.int32))
    return attended.reshape(row_total, QUERY_HEADS * HEAD_SIZE), query_diff.reshape(row_total, QUERY_HEADS * HEAD_SIZE), grad_all


def reference(tokens, queries, kv_weight, sink_logit_values, roll_offsets, out_grad):
    key_span_width = KEY_VALUE_HEADS * HEAD_SIZE

    def one_stream(weight_sum, stream_data):
        token_rows, query_rows, grad_rows, roll_start = stream_data
        projected_rows = jnp.dot(token_rows, kv_weight, preferred_element_type=jnp.float32)
        positions = (jnp.arange(SEQLEN, dtype=jnp.int32) + roll_start) % SEQLEN
        cosine_lookup, sine_lookup = rope_tables(positions)
        key_value_rotated = jnp.concatenate([apply_rotary(projected_rows[:, :key_span_width], cosine_lookup, sine_lookup, KEY_VALUE_HEADS, 1.0),
                                  projected_rows[:, key_span_width:]], axis=1).astype(jnp.bfloat16)
        query_rot = apply_rotary(query_rows.astype(jnp.float32), cosine_lookup, sine_lookup, QUERY_HEADS, 1.0).astype(jnp.bfloat16)
        keys_all = jnp.concatenate([jnp.zeros((WINDOW, 2 * key_span_width), jnp.bfloat16), key_value_rotated], axis=0)
        attended, query_diff, grad_all = band_pass(query_rot, keys_all, grad_rows, sink_logit_values, jnp.int32(0))
        local_gradient = grad_all[WINDOW:]
        query_back = apply_rotary(query_diff, cosine_lookup, sine_lookup, QUERY_HEADS, -1.0).astype(jnp.bfloat16)
        key_value_backward = jnp.concatenate([apply_rotary(local_gradient[:, :key_span_width], cosine_lookup, sine_lookup, KEY_VALUE_HEADS, -1.0),
                                   local_gradient[:, key_span_width:]], axis=1).astype(jnp.bfloat16)
        token_back = jnp.dot(key_value_backward, kv_weight.T, preferred_element_type=jnp.float32).astype(jnp.bfloat16)
        weight_part = lax.dot_general(token_rows, key_value_backward, (((0,), (0,)), ((), ())), preferred_element_type=jnp.float32)
        return weight_sum + weight_part, (attended, query_back, token_back)

    start_sum = jnp.zeros((D, 2 * key_span_width), jnp.float32)
    weight_sum, (attn_out, query_grad, token_grad) = lax.scan(one_stream, start_sum, (tokens, queries, out_grad, roll_offsets))
    weight_grad = weight_sum.reshape(N_SEQ, GRAD_BLOCK_ROWS, 128)
    return attn_out, query_grad, token_grad, weight_grad
```

```python
import jax
import jax.numpy as jnp
from jax import lax
from jax.sharding import PartitionSpec as P

QUERY_HEADS = 32
KEY_VALUE_HEADS = 4
HEAD_SIZE = 64
WINDOW = 128


rope_base = 150000.0


def from_behind(array, axis, by):
    peers = lax.axis_size(axis)
    pairs = [(i, i + by) for i in range(peers) if 0 <= i + by < peers]
    return lax.ppermute(array, axis, pairs)


def rope_tables(positions):
    half_width = HEAD_SIZE // 2
    frequency = rope_base ** (-jnp.arange(half_width, dtype=jnp.float32) / half_width)
    angle = positions.astype(jnp.float32)[:, None] * frequency[None, :]
    return (jnp.cos(angle), jnp.sin(angle))


def apply_rotary(values, cosine_lookup, sine_lookup, head_count, direction):
    row_count = values.shape[0]
    halves = values.reshape(row_count, head_count, 2, HEAD_SIZE // 2)
    front_half = halves[:, :, 0]
    back_half = halves[:, :, 1]
    cosine_rows = cosine_lookup[:, None, :]
    sine_rows = sine_lookup[:, None, :] * direction
    turned = jnp.stack(
        [
            front_half * cosine_rows - back_half * sine_rows,
            front_half * sine_rows + back_half * cosine_rows,
        ],
        axis=2,
    )
    return turned.reshape(row_count, head_count * HEAD_SIZE)


def attend_group(query_g, key_g, value_g, grad_g, sink_g, allowed):
    score_scale = HEAD_SIZE ** (-0.5)
    scores = (
        jnp.einsum("bgd,kd->gbk", query_g, key_g, preferred_element_type=jnp.float32) * score_scale
    )
    exponent = jnp.where(allowed[None], jnp.exp(scores), 0.0)
    denominator = jnp.exp(sink_g)[:, None] + jnp.sum(exponent, axis=2)
    softmax_w = exponent / denominator[:, :, None]
    softmax_b = softmax_w.astype(jnp.bfloat16)
    attended = jnp.einsum("gbk,kd->bgd", softmax_b, value_g, preferred_element_type=jnp.float32)
    dprob = jnp.einsum("bgd,kd->gbk", grad_g, value_g, preferred_element_type=jnp.float32)
    row_delta = jnp.sum(softmax_w * dprob, axis=2)
    dscore = (softmax_w * (dprob - row_delta[:, :, None]) * score_scale).astype(jnp.bfloat16)
    query_diff = jnp.einsum("gbk,kd->bgd", dscore, key_g, preferred_element_type=jnp.float32)
    key_diff = jnp.einsum("gbk,bgd->kd", dscore, query_g, preferred_element_type=jnp.float32)
    value_diff = jnp.einsum("gbk,bgd->kd", softmax_b, grad_g, preferred_element_type=jnp.float32)
    return (attended.astype(jnp.bfloat16), query_diff, key_diff, value_diff)


def attend_block(query_block, key_block, gradient_block, sink_logit_values, key_first):
    block_row_span = query_block.shape[0]
    key_row_slice = key_block.shape[0]
    group_width = QUERY_HEADS // KEY_VALUE_HEADS
    key_span_width = KEY_VALUE_HEADS * HEAD_SIZE
    rows_idx = jnp.arange(block_row_span, dtype=jnp.int32)[:, None]
    cols_idx = jnp.arange(key_row_slice, dtype=jnp.int32)[None, :]
    allowed = (cols_idx > rows_idx) & (cols_idx <= rows_idx + WINDOW) & (cols_idx + key_first >= 0)
    query_head_rows = query_block.reshape(
        block_row_span, KEY_VALUE_HEADS, group_width, HEAD_SIZE
    ).transpose(1, 0, 2, 3)
    gradient_heads = gradient_block.reshape(
        block_row_span, KEY_VALUE_HEADS, group_width, HEAD_SIZE
    ).transpose(1, 0, 2, 3)
    key_head_rows = (
        key_block[:, :key_span_width]
        .reshape(key_row_slice, KEY_VALUE_HEADS, HEAD_SIZE)
        .transpose(1, 0, 2)
    )
    value_head_rows = (
        key_block[:, key_span_width:]
        .reshape(key_row_slice, KEY_VALUE_HEADS, HEAD_SIZE)
        .transpose(1, 0, 2)
    )
    sink_per_head = sink_logit_values.reshape(KEY_VALUE_HEADS, group_width)

    def per_group(packed):
        return attend_group(packed[0], packed[1], packed[2], packed[3], packed[4], allowed)

    attended, query_diff, key_diff, value_diff = lax.map(
        per_group, (query_head_rows, key_head_rows, value_head_rows, gradient_heads, sink_per_head)
    )
    attended = attended.transpose(1, 0, 2, 3).reshape(block_row_span, QUERY_HEADS * HEAD_SIZE)
    query_diff = query_diff.transpose(1, 0, 2, 3).reshape(block_row_span, QUERY_HEADS * HEAD_SIZE)
    kv_diff = jnp.concatenate(
        [
            key_diff.transpose(1, 0, 2).reshape(key_row_slice, key_span_width),
            value_diff.transpose(1, 0, 2).reshape(key_row_slice, key_span_width),
        ],
        axis=1,
    )
    return (attended, query_diff, kv_diff)


def band_pass(query_rot, keys_all, grad_out, sink_logit_values, row_start):
    row_total = query_rot.shape[0]
    block_row_span = min(row_total, 512)

    def block_step(grad_all, block_index):
        block_begin = block_index * block_row_span
        attended, query_diff, kv_diff = attend_block(
            query_rot, keys_all, grad_out, sink_logit_values, row_start + block_begin - WINDOW
        )
        previous = grad_all
        grad_all = previous + kv_diff
        return (grad_all, (attended, query_diff))

    start_grad = jnp.zeros((row_total + WINDOW, keys_all.shape[1]), jnp.float32)
    grad_all, (attended, query_diff) = lax.scan(
        block_step, start_grad, jnp.arange(row_total // block_row_span, dtype=jnp.int32)
    )
    return (
        attended.reshape(row_total, QUERY_HEADS * HEAD_SIZE),
        query_diff.reshape(row_total, QUERY_HEADS * HEAD_SIZE),
        grad_all,
    )


FSDP_AXES = ("z", "xl", "c")
SEQ_AXES = ("xh", "y")


def gather_rows(array, axes):
    for axis in reversed(axes):
        array = lax.all_gather(array, axis, axis=0, tiled=True)
    return array


def local(tokens, queries, kv_weight, sink_logit_values, roll_offsets, out_grad):
    token_rows = tokens[0]
    query_rows = queries[0]
    grad_rows = out_grad[0]
    row_total = token_rows.shape[0]
    key_span_width = KEY_VALUE_HEADS * HEAD_SIZE
    seq_index = lax.axis_index(SEQ_AXES)
    seq_count = lax.axis_size(SEQ_AXES)
    stream_length = row_total * seq_count
    row_start = seq_index * row_total
    whole_weight = gather_rows(kv_weight, FSDP_AXES)
    feature_block = lax.all_to_all(token_rows, SEQ_AXES, split_axis=1, concat_axis=0, tiled=True)
    whole_weight, feature_block = lax.optimization_barrier((whole_weight, feature_block))
    projected_rows = jnp.dot(token_rows, whole_weight, preferred_element_type=jnp.float32)
    positions = (
        row_start + jnp.arange(row_total, dtype=jnp.int32) + roll_offsets[0]
    ) % stream_length
    cosine_lookup, sine_lookup = rope_tables(positions)
    key_value_rotated = jnp.concatenate(
        [
            apply_rotary(
                projected_rows[:, :key_span_width], cosine_lookup, sine_lookup, KEY_VALUE_HEADS, 1.0
            ),
            projected_rows[:, key_span_width:],
        ],
        axis=1,
    ).astype(jnp.bfloat16)
    query_rot = apply_rotary(
        query_rows.astype(jnp.float32), cosine_lookup, sine_lookup, QUERY_HEADS, 1.0
    ).astype(jnp.bfloat16)
    edge_rows = from_behind(key_value_rotated, SEQ_AXES, 1)
    keys_all = jnp.concatenate([edge_rows, key_value_rotated], axis=0)
    attended, query_diff, grad_all = band_pass(
        query_rot, keys_all, grad_rows, sink_logit_values, row_start
    )
    incoming = from_behind(grad_all[:WINDOW].astype(jnp.bfloat16), SEQ_AXES, -1).astype(
        jnp.float32
    )
    local_gradient = grad_all[WINDOW:]
    local_gradient = jnp.concatenate(
        [local_gradient[: row_total - WINDOW], local_gradient + incoming], axis=0
    )
    query_back = apply_rotary(query_diff, cosine_lookup, sine_lookup, QUERY_HEADS, -1.0).astype(
        jnp.bfloat16
    )
    key_value_backward = jnp.concatenate(
        [
            apply_rotary(
                local_gradient[:, :key_span_width],
                cosine_lookup,
                sine_lookup,
                KEY_VALUE_HEADS,
                -1.0,
            ),
            local_gradient[:, key_span_width:],
        ],
        axis=1,
    ).astype(jnp.bfloat16)
    token_back = lax.dot_general(
        key_value_backward,
        whole_weight,
        (((1,), (1,)), ((), ())),
        preferred_element_type=jnp.float32,
    ).astype(jnp.bfloat16)
    block_term = lax.dot_general(
        feature_block,
        gather_rows(key_value_backward, SEQ_AXES),
        (((0,), (0,)), ((), ())),
        preferred_element_type=jnp.float32,
    )
    sizes = [lax.axis_size(axis) for axis in FSDP_AXES]
    share = block_term.reshape(*sizes, -1, 128)
    for place, axis in enumerate(FSDP_AXES):
        share = lax.psum_scatter(share, axis, scatter_dimension=place, tiled=True)
    weight_share = share.reshape(-1, 128)
    return (attended[None], query_back[None], token_back[None], weight_share[None])


def solution(mesh):
    fsdp_count = mesh.shape["fsdp"]
    seq_count = mesh.shape["seq"]
    split_mesh = jax.sharding.Mesh(
        mesh.devices.reshape(fsdp_count // 4, 2, 2, 2, seq_count // 2), FSDP_AXES + SEQ_AXES
    )
    placed = (
        P(FSDP_AXES, SEQ_AXES, None),
        P(FSDP_AXES, SEQ_AXES, None),
        P(FSDP_AXES, None),
        P(),
        P(FSDP_AXES),
        P(FSDP_AXES, SEQ_AXES, None),
    )
    return jax.shard_map(
        local,
        mesh=split_mesh,
        in_specs=placed,
        out_specs=(
            P(FSDP_AXES, SEQ_AXES, None),
            P(FSDP_AXES, SEQ_AXES, None),
            P(FSDP_AXES, SEQ_AXES, None),
            P(SEQ_AXES, FSDP_AXES, None),
        ),
        check_vma=False,
    )
```

```python
import jax
import jax.numpy as jnp
from jax import lax
from jax.sharding import PartitionSpec as P

QUERY_HEADS = 32
KEY_VALUE_HEADS = 4
HEAD_SIZE = 64
WINDOW = 128


rope_base = 150000.0


def from_behind(array, axis, by):
    peers = lax.axis_size(axis)
    pairs = [(i, i + by) for i in range(peers) if 0 <= i + by < peers]
    return lax.ppermute(array, axis, pairs)


def rope_tables(positions):
    half_width = HEAD_SIZE // 2
    frequency = rope_base ** (-jnp.arange(half_width, dtype=jnp.float32) / half_width)
    angle = positions.astype(jnp.float32)[:, None] * frequency[None, :]
    return (jnp.cos(angle), jnp.sin(angle))


def apply_rotary(values, cosine_lookup, sine_lookup, head_count, direction):
    row_count = values.shape[0]
    halves = values.reshape(row_count, head_count, 2, HEAD_SIZE // 2)
    front_half = halves[:, :, 0]
    back_half = halves[:, :, 1]
    cosine_rows = cosine_lookup[:, None, :]
    sine_rows = sine_lookup[:, None, :] * direction
    turned = jnp.stack(
        [
            front_half * cosine_rows - back_half * sine_rows,
            front_half * sine_rows + back_half * cosine_rows,
        ],
        axis=2,
    )
    return turned.reshape(row_count, head_count * HEAD_SIZE)


def attend_group(query_g, key_g, value_g, grad_g, sink_g, allowed):
    score_scale = HEAD_SIZE ** (-0.5)
    scores = (
        jnp.einsum("bgd,kd->gbk", query_g, key_g, preferred_element_type=jnp.float32) * score_scale
    )
    exponent = jnp.where(allowed[None], jnp.exp(scores), 0.0)
    denominator = jnp.exp(sink_g)[:, None] + jnp.sum(exponent, axis=2)
    softmax_w = exponent / denominator[:, :, None]
    softmax_b = softmax_w.astype(jnp.bfloat16)
    attended = jnp.einsum("gbk,kd->bgd", softmax_b, value_g, preferred_element_type=jnp.float32)
    dprob = jnp.einsum("bgd,kd->gbk", grad_g, value_g, preferred_element_type=jnp.float32)
    row_delta = jnp.sum(softmax_w * dprob, axis=2)
    dscore = (softmax_w * (dprob - row_delta[:, :, None]) * score_scale).astype(jnp.bfloat16)
    query_diff = jnp.einsum("gbk,kd->bgd", dscore, key_g, preferred_element_type=jnp.float32)
    key_diff = jnp.einsum("gbk,bgd->kd", dscore, query_g, preferred_element_type=jnp.float32)
    value_diff = jnp.einsum("gbk,bgd->kd", softmax_b, grad_g, preferred_element_type=jnp.float32)
    return (attended.astype(jnp.bfloat16), query_diff, key_diff, value_diff)


def attend_block(query_block, key_block, gradient_block, sink_logit_values, key_first):
    block_row_span = query_block.shape[0]
    key_row_slice = key_block.shape[0]
    group_width = QUERY_HEADS // KEY_VALUE_HEADS
    key_span_width = KEY_VALUE_HEADS * HEAD_SIZE
    rows_idx = jnp.arange(block_row_span, dtype=jnp.int32)[:, None]
    cols_idx = jnp.arange(key_row_slice, dtype=jnp.int32)[None, :]
    allowed = (cols_idx > rows_idx) & (cols_idx <= rows_idx + WINDOW) & (cols_idx + key_first >= 0)
    query_head_rows = query_block.reshape(
        block_row_span, KEY_VALUE_HEADS, group_width, HEAD_SIZE
    ).transpose(1, 0, 2, 3)
    gradient_heads = gradient_block.reshape(
        block_row_span, KEY_VALUE_HEADS, group_width, HEAD_SIZE
    ).transpose(1, 0, 2, 3)
    key_head_rows = (
        key_block[:, :key_span_width]
        .reshape(key_row_slice, KEY_VALUE_HEADS, HEAD_SIZE)
        .transpose(1, 0, 2)
    )
    value_head_rows = (
        key_block[:, key_span_width:]
        .reshape(key_row_slice, KEY_VALUE_HEADS, HEAD_SIZE)
        .transpose(1, 0, 2)
    )
    sink_per_head = sink_logit_values.reshape(KEY_VALUE_HEADS, group_width)

    def per_group(packed):
        return attend_group(packed[0], packed[1], packed[2], packed[3], packed[4], allowed)

    attended, query_diff, key_diff, value_diff = lax.map(
        per_group, (query_head_rows, key_head_rows, value_head_rows, gradient_heads, sink_per_head)
    )
    attended = attended.transpose(1, 0, 2, 3).reshape(block_row_span, QUERY_HEADS * HEAD_SIZE)
    query_diff = query_diff.transpose(1, 0, 2, 3).reshape(block_row_span, QUERY_HEADS * HEAD_SIZE)
    kv_diff = jnp.concatenate(
        [
            key_diff.transpose(1, 0, 2).reshape(key_row_slice, key_span_width),
            value_diff.transpose(1, 0, 2).reshape(key_row_slice, key_span_width),
        ],
        axis=1,
    )
    return (attended, query_diff, kv_diff)


def band_pass(query_rot, keys_all, grad_out, sink_logit_values, row_start):
    row_total = query_rot.shape[0]
    block_row_span = min(row_total, 512)

    def block_step(grad_all, block_index):
        block_begin = block_index * block_row_span
        attended, query_diff, kv_diff = attend_block(
            query_rot, keys_all, grad_out, sink_logit_values, row_start + block_begin - WINDOW
        )
        previous = grad_all
        grad_all = previous + kv_diff
        return (grad_all, (attended, query_diff))

    start_grad = jnp.zeros((row_total + WINDOW, keys_all.shape[1]), jnp.float32)
    grad_all, (attended, query_diff) = lax.scan(
        block_step, start_grad, jnp.arange(row_total // block_row_span, dtype=jnp.int32)
    )
    return (
        attended.reshape(row_total, QUERY_HEADS * HEAD_SIZE),
        query_diff.reshape(row_total, QUERY_HEADS * HEAD_SIZE),
        grad_all,
    )


FSDP_AXES = ("z", "xl", "c")
SEQ_AXES = ("xh", "y")


def gather_by_exchange(array, axes):
    peers = lax.axis_size(axes)
    copies = jnp.broadcast_to(array[None], (peers,) + array.shape)
    copies = lax.all_to_all(copies, axes, split_axis=0, concat_axis=0, tiled=True)
    return copies.reshape(peers * array.shape[0], *array.shape[1:])


def local(tokens, queries, kv_weight, sink_logit_values, roll_offsets, out_grad):
    token_rows = tokens[0]
    query_rows = queries[0]
    grad_rows = out_grad[0]
    row_total = token_rows.shape[0]
    key_span_width = KEY_VALUE_HEADS * HEAD_SIZE
    seq_index = lax.axis_index(SEQ_AXES)
    seq_count = lax.axis_size(SEQ_AXES)
    stream_length = row_total * seq_count
    row_start = seq_index * row_total
    whole_weight = kv_weight
    for axis in FSDP_AXES:
        whole_weight = lax.all_gather(whole_weight, axis, axis=0, tiled=False)
    whole_weight = whole_weight.transpose(2, 1, 0, 3, 4).reshape(-1, whole_weight.shape[-1])
    feature_block = lax.all_to_all(token_rows, SEQ_AXES, split_axis=1, concat_axis=0, tiled=True)
    whole_weight, feature_block = lax.optimization_barrier((whole_weight, feature_block))
    projected_rows = jnp.dot(token_rows, whole_weight, preferred_element_type=jnp.float32)
    positions = (
        row_start + jnp.arange(row_total, dtype=jnp.int32) + roll_offsets[0]
    ) % stream_length
    cosine_lookup, sine_lookup = rope_tables(positions)
    key_value_rotated = jnp.concatenate(
        [
            apply_rotary(
                projected_rows[:, :key_span_width], cosine_lookup, sine_lookup, KEY_VALUE_HEADS, 1.0
            ),
            projected_rows[:, key_span_width:],
        ],
        axis=1,
    ).astype(jnp.bfloat16)
    query_rot = apply_rotary(
        query_rows.astype(jnp.float32), cosine_lookup, sine_lookup, QUERY_HEADS, 1.0
    ).astype(jnp.bfloat16)
    edge_rows = from_behind(key_value_rotated, SEQ_AXES, 1)
    keys_all = jnp.concatenate([edge_rows, key_value_rotated], axis=0)
    attended, query_diff, grad_all = band_pass(
        query_rot, keys_all, grad_rows, sink_logit_values, row_start
    )
    incoming = from_behind(grad_all[:WINDOW].astype(jnp.bfloat16), SEQ_AXES, -1).astype(
        jnp.float32
    )
    local_gradient = grad_all[WINDOW:]
    local_gradient = jnp.concatenate(
        [local_gradient[: row_total - WINDOW], local_gradient + incoming], axis=0
    )
    query_back = apply_rotary(query_diff, cosine_lookup, sine_lookup, QUERY_HEADS, -1.0).astype(
        jnp.bfloat16
    )
    key_value_backward = jnp.concatenate(
        [
            apply_rotary(
                local_gradient[:, :key_span_width],
                cosine_lookup,
                sine_lookup,
                KEY_VALUE_HEADS,
                -1.0,
            ),
            local_gradient[:, key_span_width:],
        ],
        axis=1,
    ).astype(jnp.bfloat16)
    token_back = lax.dot_general(
        key_value_backward,
        whole_weight,
        (((1,), (1,)), ((), ())),
        preferred_element_type=jnp.float32,
    ).astype(jnp.bfloat16)
    block_term = lax.dot_general(
        feature_block,
        gather_by_exchange(key_value_backward, SEQ_AXES),
        (((0,), (0,)), ((), ())),
        preferred_element_type=jnp.float32,
    )
    fsdp_count = lax.axis_size(FSDP_AXES)
    share = block_term.reshape(fsdp_count, -1, 128)
    share = lax.all_to_all(share, FSDP_AXES, split_axis=0, concat_axis=0, tiled=True)
    weight_share = jnp.sum(share, axis=0)
    return (attended[None], query_back[None], token_back[None], weight_share[None])


def solution(mesh):
    fsdp_count = mesh.shape["fsdp"]
    seq_count = mesh.shape["seq"]
    split_mesh = jax.sharding.Mesh(
        mesh.devices.reshape(fsdp_count // 4, 2, 2, 2, seq_count // 2), FSDP_AXES + SEQ_AXES
    )
    placed = (
        P(FSDP_AXES, SEQ_AXES, None),
        P(FSDP_AXES, SEQ_AXES, None),
        P(FSDP_AXES, None),
        P(),
        P(FSDP_AXES),
        P(FSDP_AXES, SEQ_AXES, None),
    )
    return jax.shard_map(
        local,
        mesh=split_mesh,
        in_specs=placed,
        out_specs=(
            P(FSDP_AXES, SEQ_AXES, None),
            P(FSDP_AXES, SEQ_AXES, None),
            P(FSDP_AXES, SEQ_AXES, None),
            P(SEQ_AXES, FSDP_AXES, None),
        ),
        check_vma=False,
    )
```

```python
import jax
import jax.numpy as jnp
from jax import lax
from jax.sharding import PartitionSpec as P

QUERY_HEADS = 32
KEY_VALUE_HEADS = 4
HEAD_SIZE = 64
WINDOW = 128


rope_base = 150000.0


def from_behind(array, axis, by):
    peers = lax.axis_size(axis)
    pairs = [(i, i + by) for i in range(peers) if 0 <= i + by < peers]
    return lax.ppermute(array, axis, pairs)


def rope_tables(positions):
    half_width = HEAD_SIZE // 2
    frequency = rope_base ** (-jnp.arange(half_width, dtype=jnp.float32) / half_width)
    angle = positions.astype(jnp.float32)[:, None] * frequency[None, :]
    return (jnp.cos(angle), jnp.sin(angle))


def apply_rotary(values, cosine_lookup, sine_lookup, head_count, direction):
    row_count = values.shape[0]
    halves = values.reshape(row_count, head_count, 2, HEAD_SIZE // 2)
    front_half = halves[:, :, 0]
    back_half = halves[:, :, 1]
    cosine_rows = cosine_lookup[:, None, :]
    sine_rows = sine_lookup[:, None, :] * direction
    turned = jnp.stack(
        [
            front_half * cosine_rows - back_half * sine_rows,
            front_half * sine_rows + back_half * cosine_rows,
        ],
        axis=2,
    )
    return turned.reshape(row_count, head_count * HEAD_SIZE)


def attend_group(query_g, key_g, value_g, grad_g, sink_g, allowed):
    score_scale = HEAD_SIZE ** (-0.5)
    scores = (
        jnp.einsum("bgd,kd->gbk", query_g, key_g, preferred_element_type=jnp.float32) * score_scale
    )
    exponent = jnp.where(allowed[None], jnp.exp(scores), 0.0)
    denominator = jnp.exp(sink_g)[:, None] + jnp.sum(exponent, axis=2)
    softmax_w = exponent / denominator[:, :, None]
    softmax_b = softmax_w.astype(jnp.bfloat16)
    attended = jnp.einsum("gbk,kd->bgd", softmax_b, value_g, preferred_element_type=jnp.float32)
    dprob = jnp.einsum("bgd,kd->gbk", grad_g, value_g, preferred_element_type=jnp.float32)
    row_delta = jnp.sum(softmax_w * dprob, axis=2)
    dscore = (softmax_w * (dprob - row_delta[:, :, None]) * score_scale).astype(jnp.bfloat16)
    query_diff = jnp.einsum("gbk,kd->bgd", dscore, key_g, preferred_element_type=jnp.float32)
    key_diff = jnp.einsum("gbk,bgd->kd", dscore, query_g, preferred_element_type=jnp.float32)
    value_diff = jnp.einsum("gbk,bgd->kd", softmax_b, grad_g, preferred_element_type=jnp.float32)
    return (attended.astype(jnp.bfloat16), query_diff, key_diff, value_diff)


def attend_block(query_block, key_block, gradient_block, sink_logit_values, key_first):
    block_row_span = query_block.shape[0]
    key_row_slice = key_block.shape[0]
    group_width = QUERY_HEADS // KEY_VALUE_HEADS
    key_span_width = KEY_VALUE_HEADS * HEAD_SIZE
    rows_idx = jnp.arange(block_row_span, dtype=jnp.int32)[:, None]
    cols_idx = jnp.arange(key_row_slice, dtype=jnp.int32)[None, :]
    allowed = (cols_idx > rows_idx) & (cols_idx <= rows_idx + WINDOW) & (cols_idx + key_first >= 0)
    query_head_rows = query_block.reshape(
        block_row_span, KEY_VALUE_HEADS, group_width, HEAD_SIZE
    ).transpose(1, 0, 2, 3)
    gradient_heads = gradient_block.reshape(
        block_row_span, KEY_VALUE_HEADS, group_width, HEAD_SIZE
    ).transpose(1, 0, 2, 3)
    key_head_rows = (
        key_block[:, :key_span_width]
        .reshape(key_row_slice, KEY_VALUE_HEADS, HEAD_SIZE)
        .transpose(1, 0, 2)
    )
    value_head_rows = (
        key_block[:, key_span_width:]
        .reshape(key_row_slice, KEY_VALUE_HEADS, HEAD_SIZE)
        .transpose(1, 0, 2)
    )
    sink_per_head = sink_logit_values.reshape(KEY_VALUE_HEADS, group_width)

    def per_group(packed):
        return attend_group(packed[0], packed[1], packed[2], packed[3], packed[4], allowed)

    attended, query_diff, key_diff, value_diff = lax.map(
        per_group, (query_head_rows, key_head_rows, value_head_rows, gradient_heads, sink_per_head)
    )
    attended = attended.transpose(1, 0, 2, 3).reshape(block_row_span, QUERY_HEADS * HEAD_SIZE)
    query_diff = query_diff.transpose(1, 0, 2, 3).reshape(block_row_span, QUERY_HEADS * HEAD_SIZE)
    kv_diff = jnp.concatenate(
        [
            key_diff.transpose(1, 0, 2).reshape(key_row_slice, key_span_width),
            value_diff.transpose(1, 0, 2).reshape(key_row_slice, key_span_width),
        ],
        axis=1,
    )
    return (attended, query_diff, kv_diff)


def band_pass(query_rot, keys_all, grad_out, sink_logit_values, row_start):
    row_total = query_rot.shape[0]
    block_row_span = min(row_total, 512)

    def block_step(grad_all, block_index):
        block_begin = block_index * block_row_span
        attended, query_diff, kv_diff = attend_block(
            query_rot, keys_all, grad_out, sink_logit_values, row_start + block_begin - WINDOW
        )
        previous = grad_all
        grad_all = previous + kv_diff
        return (grad_all, (attended, query_diff))

    start_grad = jnp.zeros((row_total + WINDOW, keys_all.shape[1]), jnp.float32)
    grad_all, (attended, query_diff) = lax.scan(
        block_step, start_grad, jnp.arange(row_total // block_row_span, dtype=jnp.int32)
    )
    return (
        attended.reshape(row_total, QUERY_HEADS * HEAD_SIZE),
        query_diff.reshape(row_total, QUERY_HEADS * HEAD_SIZE),
        grad_all,
    )


FSDP_AXES = ("z", "xl", "c")
SEQ_AXES = ("xh", "y")


def gather_by_exchange(array, axes):
    peers = lax.axis_size(axes)
    copies = jnp.broadcast_to(array[None], (peers,) + array.shape)
    copies = lax.all_to_all(copies, axes, split_axis=0, concat_axis=0, tiled=True)
    return copies.reshape(peers * array.shape[0], *array.shape[1:])


def local(tokens, queries, kv_weight, sink_logit_values, roll_offsets, out_grad):
    token_rows = tokens[0]
    query_rows = queries[0]
    grad_rows = out_grad[0]
    row_total = token_rows.shape[0]
    key_span_width = KEY_VALUE_HEADS * HEAD_SIZE
    seq_index = lax.axis_index(SEQ_AXES)
    seq_count = lax.axis_size(SEQ_AXES)
    stream_length = row_total * seq_count
    row_start = seq_index * row_total
    whole_weight = kv_weight
    for axis in reversed(FSDP_AXES):
        whole_weight = lax.all_gather(whole_weight, axis, axis=0, tiled=True)
    feature_block = lax.all_to_all(token_rows, SEQ_AXES, split_axis=1, concat_axis=0, tiled=True)
    whole_weight, feature_block = lax.optimization_barrier((whole_weight, feature_block))
    projected_rows = jnp.dot(token_rows, whole_weight, preferred_element_type=jnp.float32)
    positions = (
        row_start + jnp.arange(row_total, dtype=jnp.int32) + roll_offsets[0]
    ) % stream_length
    cosine_lookup, sine_lookup = rope_tables(positions)
    key_value_rotated = jnp.concatenate(
        [
            apply_rotary(
                projected_rows[:, :key_span_width], cosine_lookup, sine_lookup, KEY_VALUE_HEADS, 1.0
            ),
            projected_rows[:, key_span_width:],
        ],
        axis=1,
    ).astype(jnp.bfloat16)
    query_rot = apply_rotary(
        query_rows.astype(jnp.float32), cosine_lookup, sine_lookup, QUERY_HEADS, 1.0
    ).astype(jnp.bfloat16)
    edge_rows = from_behind(key_value_rotated, SEQ_AXES, 1)
    keys_all = jnp.concatenate([edge_rows, key_value_rotated], axis=0)
    attended, query_diff, grad_all = band_pass(
        query_rot, keys_all, grad_rows, sink_logit_values, row_start
    )
    incoming = from_behind(grad_all[:WINDOW].astype(jnp.bfloat16), SEQ_AXES, -1).astype(
        jnp.float32
    )
    local_gradient = grad_all[WINDOW:]
    local_gradient = jnp.concatenate(
        [local_gradient[: row_total - WINDOW], local_gradient + incoming], axis=0
    )
    query_back = apply_rotary(query_diff, cosine_lookup, sine_lookup, QUERY_HEADS, -1.0).astype(
        jnp.bfloat16
    )
    key_value_backward = jnp.concatenate(
        [
            apply_rotary(
                local_gradient[:, :key_span_width],
                cosine_lookup,
                sine_lookup,
                KEY_VALUE_HEADS,
                -1.0,
            ),
            local_gradient[:, key_span_width:],
        ],
        axis=1,
    ).astype(jnp.bfloat16)
    token_back = lax.dot_general(
        key_value_backward,
        whole_weight,
        (((1,), (1,)), ((), ())),
        preferred_element_type=jnp.float32,
    ).astype(jnp.bfloat16)
    block_term = lax.dot_general(
        feature_block,
        gather_by_exchange(key_value_backward, SEQ_AXES),
        (((0,), (0,)), ((), ())),
        preferred_element_type=jnp.float32,
    )
    fsdp_count = lax.axis_size(FSDP_AXES)
    share = block_term.reshape(fsdp_count, -1, 128)
    share = lax.all_to_all(share, FSDP_AXES, split_axis=0, concat_axis=0, tiled=True)
    weight_share = jnp.sum(share, axis=0)
    return (attended[None], query_back[None], token_back[None], weight_share[None])


def solution(mesh):
    fsdp_count = mesh.shape["fsdp"]
    seq_count = mesh.shape["seq"]
    split_mesh = jax.sharding.Mesh(
        mesh.devices.reshape(fsdp_count // 4, 2, 2, 2, seq_count // 2), FSDP_AXES + SEQ_AXES
    )
    placed = (
        P(FSDP_AXES, SEQ_AXES, None),
        P(FSDP_AXES, SEQ_AXES, None),
        P(FSDP_AXES, None),
        P(),
        P(FSDP_AXES),
        P(FSDP_AXES, SEQ_AXES, None),
    )
    return jax.shard_map(
        local,
        mesh=split_mesh,
        in_specs=placed,
        out_specs=(
            P(FSDP_AXES, SEQ_AXES, None),
            P(FSDP_AXES, SEQ_AXES, None),
            P(FSDP_AXES, SEQ_AXES, None),
            P(SEQ_AXES, FSDP_AXES, None),
        ),
        check_vma=False,
    )
```

```python
import jax
import jax.numpy as jnp
from jax import lax
from jax.sharding import PartitionSpec as P

QUERY_HEADS = 32
KEY_VALUE_HEADS = 4
HEAD_SIZE = 64
WINDOW = 128


rope_base = 150000.0


def from_behind(array, axis, by):
    peers = lax.axis_size(axis)
    pairs = [(i, i + by) for i in range(peers) if 0 <= i + by < peers]
    return lax.ppermute(array, axis, pairs)


def rope_tables(positions):
    half_width = HEAD_SIZE // 2
    frequency = rope_base ** (-jnp.arange(half_width, dtype=jnp.float32) / half_width)
    angle = positions.astype(jnp.float32)[:, None] * frequency[None, :]
    return (jnp.cos(angle), jnp.sin(angle))


def apply_rotary(values, cosine_lookup, sine_lookup, head_count, direction):
    row_count = values.shape[0]
    halves = values.reshape(row_count, head_count, 2, HEAD_SIZE // 2)
    front_half = halves[:, :, 0]
    back_half = halves[:, :, 1]
    cosine_rows = cosine_lookup[:, None, :]
    sine_rows = sine_lookup[:, None, :] * direction
    turned = jnp.stack(
        [
            front_half * cosine_rows - back_half * sine_rows,
            front_half * sine_rows + back_half * cosine_rows,
        ],
        axis=2,
    )
    return turned.reshape(row_count, head_count * HEAD_SIZE)


def attend_group(query_g, key_g, value_g, grad_g, sink_g, allowed):
    score_scale = HEAD_SIZE ** (-0.5)
    scores = (
        jnp.einsum("bgd,kd->gbk", query_g, key_g, preferred_element_type=jnp.float32) * score_scale
    )
    exponent = jnp.where(allowed[None], jnp.exp(scores), 0.0)
    denominator = jnp.exp(sink_g)[:, None] + jnp.sum(exponent, axis=2)
    softmax_w = exponent / denominator[:, :, None]
    softmax_b = softmax_w.astype(jnp.bfloat16)
    attended = jnp.einsum("gbk,kd->bgd", softmax_b, value_g, preferred_element_type=jnp.float32)
    dprob = jnp.einsum("bgd,kd->gbk", grad_g, value_g, preferred_element_type=jnp.float32)
    row_delta = jnp.sum(softmax_w * dprob, axis=2)
    dscore = (softmax_w * (dprob - row_delta[:, :, None]) * score_scale).astype(jnp.bfloat16)
    query_diff = jnp.einsum("gbk,kd->bgd", dscore, key_g, preferred_element_type=jnp.float32)
    key_diff = jnp.einsum("gbk,bgd->kd", dscore, query_g, preferred_element_type=jnp.float32)
    value_diff = jnp.einsum("gbk,bgd->kd", softmax_b, grad_g, preferred_element_type=jnp.float32)
    return (attended.astype(jnp.bfloat16), query_diff, key_diff, value_diff)


def attend_block(query_block, key_block, gradient_block, sink_logit_values, key_first):
    block_row_span = query_block.shape[0]
    key_row_slice = key_block.shape[0]
    group_width = QUERY_HEADS // KEY_VALUE_HEADS
    key_span_width = KEY_VALUE_HEADS * HEAD_SIZE
    rows_idx = jnp.arange(block_row_span, dtype=jnp.int32)[:, None]
    cols_idx = jnp.arange(key_row_slice, dtype=jnp.int32)[None, :]
    allowed = (cols_idx > rows_idx) & (cols_idx <= rows_idx + WINDOW) & (cols_idx + key_first >= 0)
    query_head_rows = query_block.reshape(
        block_row_span, KEY_VALUE_HEADS, group_width, HEAD_SIZE
    ).transpose(1, 0, 2, 3)
    gradient_heads = gradient_block.reshape(
        block_row_span, KEY_VALUE_HEADS, group_width, HEAD_SIZE
    ).transpose(1, 0, 2, 3)
    key_head_rows = (
        key_block[:, :key_span_width]
        .reshape(key_row_slice, KEY_VALUE_HEADS, HEAD_SIZE)
        .transpose(1, 0, 2)
    )
    value_head_rows = (
        key_block[:, key_span_width:]
        .reshape(key_row_slice, KEY_VALUE_HEADS, HEAD_SIZE)
        .transpose(1, 0, 2)
    )
    sink_per_head = sink_logit_values.reshape(KEY_VALUE_HEADS, group_width)

    def per_group(packed):
        return attend_group(packed[0], packed[1], packed[2], packed[3], packed[4], allowed)

    attended, query_diff, key_diff, value_diff = lax.map(
        per_group, (query_head_rows, key_head_rows, value_head_rows, gradient_heads, sink_per_head)
    )
    attended = attended.transpose(1, 0, 2, 3).reshape(block_row_span, QUERY_HEADS * HEAD_SIZE)
    query_diff = query_diff.transpose(1, 0, 2, 3).reshape(block_row_span, QUERY_HEADS * HEAD_SIZE)
    kv_diff = jnp.concatenate(
        [
            key_diff.transpose(1, 0, 2).reshape(key_row_slice, key_span_width),
            value_diff.transpose(1, 0, 2).reshape(key_row_slice, key_span_width),
        ],
        axis=1,
    )
    return (attended, query_diff, kv_diff)


def band_pass(query_rot, keys_all, grad_out, sink_logit_values, row_start):
    row_total = query_rot.shape[0]
    block_row_span = min(row_total, 512)

    def block_step(grad_all, block_index):
        block_begin = block_index * block_row_span
        attended, query_diff, kv_diff = attend_block(
            query_rot, keys_all, grad_out, sink_logit_values, row_start + block_begin - WINDOW
        )
        previous = grad_all
        grad_all = previous + kv_diff
        return (grad_all, (attended, query_diff))

    start_grad = jnp.zeros((row_total + WINDOW, keys_all.shape[1]), jnp.float32)
    grad_all, (attended, query_diff) = lax.scan(
        block_step, start_grad, jnp.arange(row_total // block_row_span, dtype=jnp.int32)
    )
    return (
        attended.reshape(row_total, QUERY_HEADS * HEAD_SIZE),
        query_diff.reshape(row_total, QUERY_HEADS * HEAD_SIZE),
        grad_all,
    )


FSDP_AXES = ("z", "xl", "c")
SEQ_AXES = ("xh", "y")


def gather_by_exchange(array, axes):
    peers = lax.axis_size(axes)
    copies = jnp.broadcast_to(array[None], (peers,) + array.shape)
    copies = lax.all_to_all(copies, axes, split_axis=0, concat_axis=0, tiled=True)
    return copies.reshape(peers * array.shape[0], *array.shape[1:])


def local(tokens, queries, kv_weight, sink_logit_values, roll_offsets, out_grad):
    token_rows = tokens[0]
    query_rows = queries[0]
    grad_rows = out_grad[0]
    row_total = token_rows.shape[0]
    key_span_width = KEY_VALUE_HEADS * HEAD_SIZE
    seq_index = lax.axis_index(SEQ_AXES)
    seq_count = lax.axis_size(SEQ_AXES)
    stream_length = row_total * seq_count
    row_start = seq_index * row_total
    whole_weight = kv_weight
    for axis in reversed(FSDP_AXES):
        whole_weight = lax.all_gather(whole_weight, axis, axis=0, tiled=True)
    feature_block = lax.all_to_all(token_rows, SEQ_AXES, split_axis=1, concat_axis=0, tiled=True)
    whole_weight, feature_block = lax.optimization_barrier((whole_weight, feature_block))
    projected_rows = jnp.dot(token_rows, whole_weight, preferred_element_type=jnp.float32)
    positions = (
        row_start + jnp.arange(row_total, dtype=jnp.int32) + roll_offsets[0]
    ) % stream_length
    cosine_lookup, sine_lookup = rope_tables(positions)
    key_value_rotated = jnp.concatenate(
        [
            apply_rotary(
                projected_rows[:, :key_span_width], cosine_lookup, sine_lookup, KEY_VALUE_HEADS, 1.0
            ),
            projected_rows[:, key_span_width:],
        ],
        axis=1,
    ).astype(jnp.bfloat16)
    query_rot = apply_rotary(
        query_rows.astype(jnp.float32), cosine_lookup, sine_lookup, QUERY_HEADS, 1.0
    ).astype(jnp.bfloat16)
    edge_rows = from_behind(key_value_rotated, SEQ_AXES, 1)
    keys_all = jnp.concatenate([edge_rows, key_value_rotated], axis=0)
    attended, query_diff, grad_all = band_pass(
        query_rot, keys_all, grad_rows, sink_logit_values, row_start
    )
    incoming = from_behind(grad_all[:WINDOW].astype(jnp.bfloat16), SEQ_AXES, -1).astype(
        jnp.float32
    )
    local_gradient = grad_all[WINDOW:]
    local_gradient = jnp.concatenate(
        [local_gradient[: row_total - WINDOW], local_gradient + incoming], axis=0
    )
    query_back = apply_rotary(query_diff, cosine_lookup, sine_lookup, QUERY_HEADS, -1.0).astype(
        jnp.bfloat16
    )
    key_value_backward = jnp.concatenate(
        [
            apply_rotary(
                local_gradient[:, :key_span_width],
                cosine_lookup,
                sine_lookup,
                KEY_VALUE_HEADS,
                -1.0,
            ),
            local_gradient[:, key_span_width:],
        ],
        axis=1,
    ).astype(jnp.bfloat16)
    token_back = lax.dot_general(
        key_value_backward,
        whole_weight,
        (((1,), (1,)), ((), ())),
        preferred_element_type=jnp.float32,
    ).astype(jnp.bfloat16)
    block_term = lax.dot_general(
        feature_block,
        gather_by_exchange(gather_by_exchange(key_value_backward, SEQ_AXES[1:]), SEQ_AXES[:1]),
        (((0,), (0,)), ((), ())),
        preferred_element_type=jnp.float32,
    )
    fsdp_count = lax.axis_size(FSDP_AXES)
    share = block_term.reshape(fsdp_count, -1, 128)
    share = lax.all_to_all(share, FSDP_AXES, split_axis=0, concat_axis=0, tiled=True)
    weight_share = jnp.sum(share, axis=0)
    return (attended[None], query_back[None], token_back[None], weight_share[None])


def solution(mesh):
    fsdp_count = mesh.shape["fsdp"]
    seq_count = mesh.shape["seq"]
    split_mesh = jax.sharding.Mesh(
        mesh.devices.reshape(fsdp_count // 4, 2, 2, 2, seq_count // 2), FSDP_AXES + SEQ_AXES
    )
    placed = (
        P(FSDP_AXES, SEQ_AXES, None),
        P(FSDP_AXES, SEQ_AXES, None),
        P(FSDP_AXES, None),
        P(),
        P(FSDP_AXES),
        P(FSDP_AXES, SEQ_AXES, None),
    )
    return jax.shard_map(
        local,
        mesh=split_mesh,
        in_specs=placed,
        out_specs=(
            P(FSDP_AXES, SEQ_AXES, None),
            P(FSDP_AXES, SEQ_AXES, None),
            P(FSDP_AXES, SEQ_AXES, None),
            P(SEQ_AXES, FSDP_AXES, None),
        ),
        check_vma=False,
    )
```

```python
import jax
import jax.numpy as jnp
from jax import lax
from jax.experimental import pallas as pl
from jax.experimental.pallas import tpu as pltpu
from jax.sharding import PartitionSpec as P

QUERY_HEADS = 32
KEY_VALUE_HEADS = 4
HEAD_SIZE = 64
WINDOW = 128


rope_base = 150000.0


def from_behind(array, axis, by):
    peers = lax.axis_size(axis)
    pairs = [(i, i + by) for i in range(peers) if 0 <= i + by < peers]
    return lax.ppermute(array, axis, pairs)


def rope_tables(positions):
    half_width = HEAD_SIZE // 2
    frequency = rope_base ** (-jnp.arange(half_width, dtype=jnp.float32) / half_width)
    angle = positions.astype(jnp.float32)[:, None] * frequency[None, :]
    return (jnp.cos(angle), jnp.sin(angle))


def apply_rotary(values, cosine_lookup, sine_lookup, head_count, direction):
    row_count = values.shape[0]
    halves = values.reshape(row_count, head_count, 2, HEAD_SIZE // 2)
    front_half = halves[:, :, 0]
    back_half = halves[:, :, 1]
    cosine_rows = cosine_lookup[:, None, :]
    sine_rows = sine_lookup[:, None, :] * direction
    turned = jnp.stack(
        [
            front_half * cosine_rows - back_half * sine_rows,
            front_half * sine_rows + back_half * cosine_rows,
        ],
        axis=2,
    )
    return turned.reshape(row_count, head_count * HEAD_SIZE)


def band_kernel(sink_ref, lead_ref, q_ref, g_ref, k_ref, v_ref, attn_ref, dq_ref, dk_ref, dv_ref):
    score_scale = HEAD_SIZE ** (-0.5)
    group_width = QUERY_HEADS // KEY_VALUE_HEADS
    row_count = q_ref.shape[1]
    key_count = k_ref.shape[1]
    rows = lax.broadcasted_iota(jnp.int32, (row_count, key_count), 0)
    cols = lax.broadcasted_iota(jnp.int32, (row_count, key_count), 1)
    allowed = (cols > rows) & (cols <= rows + WINDOW) & (cols >= lead_ref[0])
    trans_a = (((0,), (0,)), ((), ()))
    trans_b = (((1,), (1,)), ((), ()))
    for group in range(KEY_VALUE_HEADS):
        key_g = k_ref[group]
        value_g = v_ref[group]

        def head_step(member, carry):
            key_acc, value_acc = carry
            head = group * group_width + member
            query_h = q_ref[head]
            grad_h = g_ref[head]
            scores = (
                lax.dot_general(query_h, key_g, trans_b, preferred_element_type=jnp.float32)
                * score_scale
            )
            exponent = jnp.where(allowed, jnp.exp(scores), 0.0)
            denominator = sink_ref[head] + jnp.sum(exponent, axis=1, keepdims=True)
            softmax_w = exponent / denominator
            softmax_b = softmax_w.astype(jnp.bfloat16)
            attn_ref[head] = jnp.dot(
                softmax_b, value_g, preferred_element_type=jnp.float32
            ).astype(jnp.bfloat16)
            dprob = lax.dot_general(grad_h, value_g, trans_b, preferred_element_type=jnp.float32)
            row_delta = jnp.sum(softmax_w * dprob, axis=1, keepdims=True)
            dscore = (softmax_w * (dprob - row_delta) * score_scale).astype(jnp.bfloat16)
            dq_ref[head] = jnp.dot(dscore, key_g, preferred_element_type=jnp.float32)
            key_acc = key_acc + lax.dot_general(
                dscore, query_h, trans_a, preferred_element_type=jnp.float32
            )
            value_acc = value_acc + lax.dot_general(
                softmax_b, grad_h, trans_a, preferred_element_type=jnp.float32
            )
            return key_acc, value_acc

        start = jnp.zeros((key_count, HEAD_SIZE), jnp.float32)
        key_acc, value_acc = lax.fori_loop(0, group_width, head_step, (start, start))
        dk_ref[group] = key_acc
        dv_ref[group] = value_acc


def band_attention(query_rot, keys_all, grad_out, sink_logit_values, row_start):
    row_total = query_rot.shape[0]
    key_total = keys_all.shape[0]
    key_span_width = KEY_VALUE_HEADS * HEAD_SIZE
    q_heads = query_rot.reshape(row_total, QUERY_HEADS, HEAD_SIZE).transpose(1, 0, 2)
    g_heads = grad_out.reshape(row_total, QUERY_HEADS, HEAD_SIZE).transpose(1, 0, 2)
    k_heads = (
        keys_all[:, :key_span_width].reshape(key_total, KEY_VALUE_HEADS, HEAD_SIZE).transpose(1, 0, 2)
    )
    v_heads = (
        keys_all[:, key_span_width:].reshape(key_total, KEY_VALUE_HEADS, HEAD_SIZE).transpose(1, 0, 2)
    )
    sink_weight = jnp.exp(sink_logit_values)
    lead = jnp.maximum(WINDOW - row_start, 0).astype(jnp.int32).reshape(1)
    smem = pl.BlockSpec(memory_space=pltpu.SMEM)
    vmem = pl.BlockSpec(memory_space=pltpu.VMEM)
    attn_h, dq_h, dk_h, dv_h = pl.pallas_call(
        band_kernel,
        out_shape=(
            jax.ShapeDtypeStruct(q_heads.shape, jnp.bfloat16),
            jax.ShapeDtypeStruct(q_heads.shape, jnp.float32),
            jax.ShapeDtypeStruct(k_heads.shape, jnp.float32),
            jax.ShapeDtypeStruct(k_heads.shape, jnp.float32),
        ),
        in_specs=[smem, smem, vmem, vmem, vmem, vmem],
        out_specs=(vmem, vmem, vmem, vmem),
    )(sink_weight, lead, q_heads, g_heads, k_heads, v_heads)
    attended = attn_h.transpose(1, 0, 2).reshape(row_total, QUERY_HEADS * HEAD_SIZE)
    query_diff = dq_h.transpose(1, 0, 2).reshape(row_total, QUERY_HEADS * HEAD_SIZE)
    kv_diff = jnp.concatenate(
        [
            dk_h.transpose(1, 0, 2).reshape(key_total, key_span_width),
            dv_h.transpose(1, 0, 2).reshape(key_total, key_span_width),
        ],
        axis=1,
    )
    return attended, query_diff, kv_diff


FSDP_AXES = ("z", "xl", "c")
SEQ_AXES = ("xh", "y")


def gather_by_exchange(array, axes):
    peers = lax.axis_size(axes)
    copies = jnp.broadcast_to(array[None], (peers,) + array.shape)
    copies = lax.all_to_all(copies, axes, split_axis=0, concat_axis=0, tiled=True)
    return copies.reshape(peers * array.shape[0], *array.shape[1:])


def local(tokens, queries, kv_weight, sink_logit_values, roll_offsets, out_grad):
    token_rows = tokens[0]
    query_rows = queries[0]
    grad_rows = out_grad[0]
    row_total = token_rows.shape[0]
    key_span_width = KEY_VALUE_HEADS * HEAD_SIZE
    seq_index = lax.axis_index(SEQ_AXES)
    seq_count = lax.axis_size(SEQ_AXES)
    stream_length = row_total * seq_count
    row_start = seq_index * row_total
    whole_weight = kv_weight
    for axis in reversed(FSDP_AXES):
        whole_weight = lax.all_gather(whole_weight, axis, axis=0, tiled=True)
    feature_block = lax.all_to_all(token_rows, SEQ_AXES, split_axis=1, concat_axis=0, tiled=True)
    whole_weight, feature_block = lax.optimization_barrier((whole_weight, feature_block))
    projected_rows = jnp.dot(token_rows, whole_weight, preferred_element_type=jnp.float32)
    positions = (
        row_start + jnp.arange(row_total, dtype=jnp.int32) + roll_offsets[0]
    ) % stream_length
    cosine_lookup, sine_lookup = rope_tables(positions)
    key_value_rotated = jnp.concatenate(
        [
            apply_rotary(
                projected_rows[:, :key_span_width], cosine_lookup, sine_lookup, KEY_VALUE_HEADS, 1.0
            ),
            projected_rows[:, key_span_width:],
        ],
        axis=1,
    ).astype(jnp.bfloat16)
    query_rot = apply_rotary(
        query_rows.astype(jnp.float32), cosine_lookup, sine_lookup, QUERY_HEADS, 1.0
    ).astype(jnp.bfloat16)
    edge_rows = from_behind(key_value_rotated, SEQ_AXES, 1)
    keys_all = jnp.concatenate([edge_rows, key_value_rotated], axis=0)
    attended, query_diff, grad_all = band_attention(
        query_rot, keys_all, grad_rows, sink_logit_values, row_start
    )
    incoming = from_behind(grad_all[:WINDOW].astype(jnp.bfloat16), SEQ_AXES, -1).astype(
        jnp.float32
    )
    local_gradient = grad_all[WINDOW:]
    local_gradient = jnp.concatenate(
        [local_gradient[: row_total - WINDOW], local_gradient + incoming], axis=0
    )
    query_back = apply_rotary(query_diff, cosine_lookup, sine_lookup, QUERY_HEADS, -1.0).astype(
        jnp.bfloat16
    )
    key_value_backward = jnp.concatenate(
        [
            apply_rotary(
                local_gradient[:, :key_span_width],
                cosine_lookup,
                sine_lookup,
                KEY_VALUE_HEADS,
                -1.0,
            ),
            local_gradient[:, key_span_width:],
        ],
        axis=1,
    ).astype(jnp.bfloat16)
    token_back = lax.dot_general(
        key_value_backward,
        whole_weight,
        (((1,), (1,)), ((), ())),
        preferred_element_type=jnp.float32,
    ).astype(jnp.bfloat16)
    block_term = lax.dot_general(
        feature_block,
        gather_by_exchange(gather_by_exchange(key_value_backward, SEQ_AXES[1:]), SEQ_AXES[:1]),
        (((0,), (0,)), ((), ())),
        preferred_element_type=jnp.float32,
    )
    fsdp_count = lax.axis_size(FSDP_AXES)
    share = block_term.reshape(fsdp_count, -1, 128)
    share = lax.all_to_all(share, FSDP_AXES, split_axis=0, concat_axis=0, tiled=True)
    weight_share = jnp.sum(share, axis=0)
    return (attended[None], query_back[None], token_back[None], weight_share[None])


def solution(mesh):
    fsdp_count = mesh.shape["fsdp"]
    seq_count = mesh.shape["seq"]
    split_mesh = jax.sharding.Mesh(
        mesh.devices.reshape(fsdp_count // 4, 2, 2, 2, seq_count // 2), FSDP_AXES + SEQ_AXES
    )
    placed = (
        P(FSDP_AXES, SEQ_AXES, None),
        P(FSDP_AXES, SEQ_AXES, None),
        P(FSDP_AXES, None),
        P(),
        P(FSDP_AXES),
        P(FSDP_AXES, SEQ_AXES, None),
    )
    return jax.shard_map(
        local,
        mesh=split_mesh,
        in_specs=placed,
        out_specs=(
            P(FSDP_AXES, SEQ_AXES, None),
            P(FSDP_AXES, SEQ_AXES, None),
            P(FSDP_AXES, SEQ_AXES, None),
            P(SEQ_AXES, FSDP_AXES, None),
        ),
        check_vma=False,
    )
```

```python
import jax
import jax.numpy as jnp
from jax import lax
from jax.experimental import pallas as pl
from jax.experimental.pallas import tpu as pltpu
from jax.sharding import PartitionSpec as P

QUERY_HEADS = 32
KEY_VALUE_HEADS = 4
HEAD_SIZE = 64
WINDOW = 128


rope_base = 150000.0


def from_behind(array, axis, by):
    peers = lax.axis_size(axis)
    pairs = [(i, i + by) for i in range(peers) if 0 <= i + by < peers]
    return lax.ppermute(array, axis, pairs)


def rope_tables(positions):
    half_width = HEAD_SIZE // 2
    frequency = rope_base ** (-jnp.arange(half_width, dtype=jnp.float32) / half_width)
    angle = positions.astype(jnp.float32)[:, None] * frequency[None, :]
    return (jnp.cos(angle), jnp.sin(angle))


def apply_rotary(values, cosine_lookup, sine_lookup, head_count, direction):
    row_count = values.shape[0]
    halves = values.reshape(row_count, head_count, 2, HEAD_SIZE // 2)
    front_half = halves[:, :, 0]
    back_half = halves[:, :, 1]
    cosine_rows = cosine_lookup[:, None, :]
    sine_rows = sine_lookup[:, None, :] * direction
    turned = jnp.stack(
        [
            front_half * cosine_rows - back_half * sine_rows,
            front_half * sine_rows + back_half * cosine_rows,
        ],
        axis=2,
    )
    return turned.reshape(row_count, head_count * HEAD_SIZE)


def band_kernel(sink_ref, lead_ref, q_ref, g_ref, k_ref, v_ref, attn_ref, dq_ref, dk_ref, dv_ref):
    score_scale = HEAD_SIZE ** (-0.5)
    group_width = QUERY_HEADS // KEY_VALUE_HEADS
    row_count = q_ref.shape[1]
    key_count = k_ref.shape[1]
    rows = lax.broadcasted_iota(jnp.int32, (row_count, key_count), 0)
    cols = lax.broadcasted_iota(jnp.int32, (row_count, key_count), 1)
    allowed = (cols > rows) & (cols <= rows + WINDOW) & (cols >= lead_ref[0])
    trans_a = (((0,), (0,)), ((), ()))
    trans_b = (((1,), (1,)), ((), ()))
    for group in range(KEY_VALUE_HEADS):
        key_g = k_ref[group]
        value_g = v_ref[group]

        def head_step(member, carry):
            key_acc, value_acc = carry
            head = group * group_width + member
            query_h = q_ref[head]
            grad_h = g_ref[head]
            scores = (
                lax.dot_general(query_h, key_g, trans_b, preferred_element_type=jnp.float32)
                * score_scale
            )
            exponent = jnp.where(allowed, jnp.exp(scores), 0.0)
            denominator = sink_ref[head] + jnp.sum(exponent, axis=1, keepdims=True)
            softmax_w = exponent / denominator
            softmax_b = softmax_w.astype(jnp.bfloat16)
            attn_ref[head] = jnp.dot(
                softmax_b, value_g, preferred_element_type=jnp.float32
            ).astype(jnp.bfloat16)
            dprob = lax.dot_general(grad_h, value_g, trans_b, preferred_element_type=jnp.float32)
            row_delta = jnp.sum(softmax_w * dprob, axis=1, keepdims=True)
            dscore = (softmax_w * (dprob - row_delta) * score_scale).astype(jnp.bfloat16)
            dq_ref[head] = jnp.dot(dscore, key_g, preferred_element_type=jnp.float32)
            key_acc = key_acc + lax.dot_general(
                dscore, query_h, trans_a, preferred_element_type=jnp.float32
            )
            value_acc = value_acc + lax.dot_general(
                softmax_b, grad_h, trans_a, preferred_element_type=jnp.float32
            )
            return key_acc, value_acc

        start = jnp.zeros((key_count, HEAD_SIZE), jnp.float32)
        key_acc, value_acc = lax.fori_loop(
            0, group_width, head_step, (start, start), unroll=True
        )
        dk_ref[group] = key_acc
        dv_ref[group] = value_acc


def band_attention(query_rot, keys_all, grad_out, sink_logit_values, row_start):
    row_total = query_rot.shape[0]
    key_total = keys_all.shape[0]
    key_span_width = KEY_VALUE_HEADS * HEAD_SIZE
    q_heads = query_rot.reshape(row_total, QUERY_HEADS, HEAD_SIZE).transpose(1, 0, 2)
    g_heads = grad_out.reshape(row_total, QUERY_HEADS, HEAD_SIZE).transpose(1, 0, 2)
    k_heads = (
        keys_all[:, :key_span_width].reshape(key_total, KEY_VALUE_HEADS, HEAD_SIZE).transpose(1, 0, 2)
    )
    v_heads = (
        keys_all[:, key_span_width:].reshape(key_total, KEY_VALUE_HEADS, HEAD_SIZE).transpose(1, 0, 2)
    )
    sink_weight = jnp.exp(sink_logit_values)
    lead = jnp.maximum(WINDOW - row_start, 0).astype(jnp.int32).reshape(1)
    smem = pl.BlockSpec(memory_space=pltpu.SMEM)
    vmem = pl.BlockSpec(memory_space=pltpu.VMEM)
    attn_h, dq_h, dk_h, dv_h = pl.pallas_call(
        band_kernel,
        out_shape=(
            jax.ShapeDtypeStruct(q_heads.shape, jnp.bfloat16),
            jax.ShapeDtypeStruct(q_heads.shape, jnp.float32),
            jax.ShapeDtypeStruct(k_heads.shape, jnp.float32),
            jax.ShapeDtypeStruct(k_heads.shape, jnp.float32),
        ),
        in_specs=[smem, smem, vmem, vmem, vmem, vmem],
        out_specs=(vmem, vmem, vmem, vmem),
    )(sink_weight, lead, q_heads, g_heads, k_heads, v_heads)
    attended = attn_h.transpose(1, 0, 2).reshape(row_total, QUERY_HEADS * HEAD_SIZE)
    query_diff = dq_h.transpose(1, 0, 2).reshape(row_total, QUERY_HEADS * HEAD_SIZE)
    kv_diff = jnp.concatenate(
        [
            dk_h.transpose(1, 0, 2).reshape(key_total, key_span_width),
            dv_h.transpose(1, 0, 2).reshape(key_total, key_span_width),
        ],
        axis=1,
    )
    return attended, query_diff, kv_diff


FSDP_AXES = ("z", "xl", "c")
SEQ_AXES = ("xh", "y")


def gather_by_exchange(array, axes):
    peers = lax.axis_size(axes)
    copies = jnp.broadcast_to(array[None], (peers,) + array.shape)
    copies = lax.all_to_all(copies, axes, split_axis=0, concat_axis=0, tiled=True)
    return copies.reshape(peers * array.shape[0], *array.shape[1:])


def local(tokens, queries, kv_weight, sink_logit_values, roll_offsets, out_grad):
    token_rows = tokens[0]
    query_rows = queries[0]
    grad_rows = out_grad[0]
    row_total = token_rows.shape[0]
    key_span_width = KEY_VALUE_HEADS * HEAD_SIZE
    seq_index = lax.axis_index(SEQ_AXES)
    seq_count = lax.axis_size(SEQ_AXES)
    stream_length = row_total * seq_count
    row_start = seq_index * row_total
    whole_weight = kv_weight
    for axis in reversed(FSDP_AXES):
        whole_weight = lax.all_gather(whole_weight, axis, axis=0, tiled=True)
    feature_block = lax.all_to_all(token_rows, SEQ_AXES, split_axis=1, concat_axis=0, tiled=True)
    whole_weight, feature_block = lax.optimization_barrier((whole_weight, feature_block))
    projected_rows = jnp.dot(token_rows, whole_weight, preferred_element_type=jnp.float32)
    positions = (
        row_start + jnp.arange(row_total, dtype=jnp.int32) + roll_offsets[0]
    ) % stream_length
    cosine_lookup, sine_lookup = rope_tables(positions)
    key_value_rotated = jnp.concatenate(
        [
            apply_rotary(
                projected_rows[:, :key_span_width], cosine_lookup, sine_lookup, KEY_VALUE_HEADS, 1.0
            ),
            projected_rows[:, key_span_width:],
        ],
        axis=1,
    ).astype(jnp.bfloat16)
    query_rot = apply_rotary(
        query_rows.astype(jnp.float32), cosine_lookup, sine_lookup, QUERY_HEADS, 1.0
    ).astype(jnp.bfloat16)
    edge_rows = from_behind(key_value_rotated, SEQ_AXES, 1)
    keys_all = jnp.concatenate([edge_rows, key_value_rotated], axis=0)
    attended, query_diff, grad_all = band_attention(
        query_rot, keys_all, grad_rows, sink_logit_values, row_start
    )
    incoming = from_behind(grad_all[:WINDOW].astype(jnp.bfloat16), SEQ_AXES, -1).astype(
        jnp.float32
    )
    local_gradient = grad_all[WINDOW:]
    local_gradient = jnp.concatenate(
        [local_gradient[: row_total - WINDOW], local_gradient + incoming], axis=0
    )
    query_back = apply_rotary(query_diff, cosine_lookup, sine_lookup, QUERY_HEADS, -1.0).astype(
        jnp.bfloat16
    )
    key_value_backward = jnp.concatenate(
        [
            apply_rotary(
                local_gradient[:, :key_span_width],
                cosine_lookup,
                sine_lookup,
                KEY_VALUE_HEADS,
                -1.0,
            ),
            local_gradient[:, key_span_width:],
        ],
        axis=1,
    ).astype(jnp.bfloat16)
    token_back = lax.dot_general(
        key_value_backward,
        whole_weight,
        (((1,), (1,)), ((), ())),
        preferred_element_type=jnp.float32,
    ).astype(jnp.bfloat16)
    block_term = lax.dot_general(
        feature_block,
        gather_by_exchange(gather_by_exchange(key_value_backward, SEQ_AXES[1:]), SEQ_AXES[:1]),
        (((0,), (0,)), ((), ())),
        preferred_element_type=jnp.float32,
    )
    fsdp_count = lax.axis_size(FSDP_AXES)
    share = block_term.reshape(fsdp_count, -1, 128)
    share = lax.all_to_all(share, FSDP_AXES, split_axis=0, concat_axis=0, tiled=True)
    weight_share = jnp.sum(share, axis=0)
    return (attended[None], query_back[None], token_back[None], weight_share[None])


def solution(mesh):
    fsdp_count = mesh.shape["fsdp"]
    seq_count = mesh.shape["seq"]
    split_mesh = jax.sharding.Mesh(
        mesh.devices.reshape(fsdp_count // 4, 2, 2, 2, seq_count // 2), FSDP_AXES + SEQ_AXES
    )
    placed = (
        P(FSDP_AXES, SEQ_AXES, None),
        P(FSDP_AXES, SEQ_AXES, None),
        P(FSDP_AXES, None),
        P(),
        P(FSDP_AXES),
        P(FSDP_AXES, SEQ_AXES, None),
    )
    return jax.shard_map(
        local,
        mesh=split_mesh,
        in_specs=placed,
        out_specs=(
            P(FSDP_AXES, SEQ_AXES, None),
            P(FSDP_AXES, SEQ_AXES, None),
            P(FSDP_AXES, SEQ_AXES, None),
            P(SEQ_AXES, FSDP_AXES, None),
        ),
        check_vma=False,
    )
```

```python
import jax
import jax.numpy as jnp
from jax import lax
from jax.experimental import pallas as pl
from jax.experimental.pallas import tpu as pltpu
from jax.sharding import PartitionSpec as P

QUERY_HEADS = 32
KEY_VALUE_HEADS = 4
HEAD_SIZE = 64
WINDOW = 128


rope_base = 150000.0


def from_behind(array, axis, by):
    peers = lax.axis_size(axis)
    pairs = [(i, i + by) for i in range(peers) if 0 <= i + by < peers]
    return lax.ppermute(array, axis, pairs)


def rope_tables(positions):
    half_width = HEAD_SIZE // 2
    frequency = rope_base ** (-jnp.arange(half_width, dtype=jnp.float32) / half_width)
    angle = positions.astype(jnp.float32)[:, None] * frequency[None, :]
    return (jnp.cos(angle), jnp.sin(angle))


def apply_rotary(values, cosine_lookup, sine_lookup, head_count, direction):
    row_count = values.shape[0]
    halves = values.reshape(row_count, head_count, 2, HEAD_SIZE // 2)
    front_half = halves[:, :, 0]
    back_half = halves[:, :, 1]
    cosine_rows = cosine_lookup[:, None, :]
    sine_rows = sine_lookup[:, None, :] * direction
    turned = jnp.stack(
        [
            front_half * cosine_rows - back_half * sine_rows,
            front_half * sine_rows + back_half * cosine_rows,
        ],
        axis=2,
    )
    return turned.reshape(row_count, head_count * HEAD_SIZE)


def band_kernel(sink_ref, lead_ref, q_ref, g_ref, k_ref, v_ref, attn_ref, dq_ref, dk_ref, dv_ref):
    score_scale = HEAD_SIZE ** (-0.5)
    group_width = QUERY_HEADS // KEY_VALUE_HEADS
    row_count = q_ref.shape[1]
    key_count = k_ref.shape[1]
    rows = lax.broadcasted_iota(jnp.int32, (row_count, key_count), 0)
    cols = lax.broadcasted_iota(jnp.int32, (row_count, key_count), 1)
    allowed = (cols > rows) & (cols <= rows + WINDOW) & (cols >= lead_ref[0])
    trans_a = (((0,), (0,)), ((), ()))
    trans_b = (((1,), (1,)), ((), ()))
    for group in range(KEY_VALUE_HEADS):
        key_g = k_ref[group]
        value_g = v_ref[group]

        def head_step(member, carry):
            key_acc, value_acc = carry
            head = group * group_width + member
            query_h = q_ref[head]
            grad_h = g_ref[head]
            scores = (
                lax.dot_general(query_h, key_g, trans_b, preferred_element_type=jnp.float32)
                * score_scale
            )
            exponent = jnp.where(allowed, jnp.exp(scores), 0.0)
            denominator = sink_ref[head] + jnp.sum(exponent, axis=1, keepdims=True)
            softmax_w = exponent / denominator
            softmax_b = softmax_w.astype(jnp.bfloat16)
            attn_ref[head] = jnp.dot(
                softmax_b, value_g, preferred_element_type=jnp.float32
            ).astype(jnp.bfloat16)
            dprob = lax.dot_general(grad_h, value_g, trans_b, preferred_element_type=jnp.float32)
            row_delta = jnp.sum(softmax_w * dprob, axis=1, keepdims=True)
            dscore = (softmax_w * (dprob - row_delta) * score_scale).astype(jnp.bfloat16)
            dq_ref[head] = jnp.dot(dscore, key_g, preferred_element_type=jnp.float32)
            key_acc = key_acc + lax.dot_general(
                dscore, query_h, trans_a, preferred_element_type=jnp.float32
            )
            value_acc = value_acc + lax.dot_general(
                softmax_b, grad_h, trans_a, preferred_element_type=jnp.float32
            )
            return key_acc, value_acc

        start = jnp.zeros((key_count, HEAD_SIZE), jnp.float32)
        key_acc, value_acc = lax.fori_loop(
            0, group_width, head_step, (start, start), unroll=True
        )
        dk_ref[group] = key_acc
        dv_ref[group] = value_acc


def band_attention(query_rot, keys_all, grad_out, sink_logit_values, row_start):
    row_total = query_rot.shape[0]
    key_total = keys_all.shape[0]
    key_span_width = KEY_VALUE_HEADS * HEAD_SIZE
    q_heads = query_rot.reshape(row_total, QUERY_HEADS, HEAD_SIZE).transpose(1, 0, 2)
    g_heads = grad_out.reshape(row_total, QUERY_HEADS, HEAD_SIZE).transpose(1, 0, 2)
    k_heads = (
        keys_all[:, :key_span_width].reshape(key_total, KEY_VALUE_HEADS, HEAD_SIZE).transpose(1, 0, 2)
    )
    v_heads = (
        keys_all[:, key_span_width:].reshape(key_total, KEY_VALUE_HEADS, HEAD_SIZE).transpose(1, 0, 2)
    )
    sink_weight = jnp.exp(sink_logit_values)
    lead = jnp.maximum(WINDOW - row_start, 0).astype(jnp.int32).reshape(1)
    smem = pl.BlockSpec(memory_space=pltpu.SMEM)
    vmem = pl.BlockSpec(memory_space=pltpu.VMEM)
    attn_h, dq_h, dk_h, dv_h = pl.pallas_call(
        band_kernel,
        out_shape=(
            jax.ShapeDtypeStruct(q_heads.shape, jnp.bfloat16),
            jax.ShapeDtypeStruct(q_heads.shape, jnp.float32),
            jax.ShapeDtypeStruct(k_heads.shape, jnp.float32),
            jax.ShapeDtypeStruct(k_heads.shape, jnp.float32),
        ),
        in_specs=[smem, smem, vmem, vmem, vmem, vmem],
        out_specs=(vmem, vmem, vmem, vmem),
    )(sink_weight, lead, q_heads, g_heads, k_heads, v_heads)
    attended = attn_h.transpose(1, 0, 2).reshape(row_total, QUERY_HEADS * HEAD_SIZE)
    query_diff = dq_h.transpose(1, 0, 2).reshape(row_total, QUERY_HEADS * HEAD_SIZE)
    kv_diff = jnp.concatenate(
        [
            dk_h.transpose(1, 0, 2).reshape(key_total, key_span_width),
            dv_h.transpose(1, 0, 2).reshape(key_total, key_span_width),
        ],
        axis=1,
    )
    return attended, query_diff, kv_diff


FSDP_AXES = ("z", "xl", "c")
SEQ_AXES = ("xh", "y")


def gather_by_exchange(array, axes):
    peers = lax.axis_size(axes)
    copies = jnp.broadcast_to(array[None], (peers,) + array.shape)
    copies = lax.all_to_all(copies, axes, split_axis=0, concat_axis=0, tiled=True)
    return copies.reshape(peers * array.shape[0], *array.shape[1:])


def local(tokens, queries, kv_weight, sink_logit_values, roll_offsets, out_grad):
    token_rows = tokens[0]
    query_rows = queries[0]
    grad_rows = out_grad[0]
    row_total = token_rows.shape[0]
    key_span_width = KEY_VALUE_HEADS * HEAD_SIZE
    seq_index = lax.axis_index(SEQ_AXES)
    seq_count = lax.axis_size(SEQ_AXES)
    stream_length = row_total * seq_count
    row_start = seq_index * row_total
    split_at = kv_weight.shape[1] * 3 // 4
    offload_part = kv_weight[:, :split_at]
    for axis in reversed(FSDP_AXES):
        offload_part = lax.all_gather(offload_part, axis, axis=0, tiled=True)
    exchange_part = gather_by_exchange(kv_weight[:, split_at:], FSDP_AXES)
    whole_weight = jnp.concatenate([offload_part, exchange_part], axis=1)
    feature_block = lax.all_to_all(token_rows, SEQ_AXES, split_axis=1, concat_axis=0, tiled=True)
    whole_weight, feature_block = lax.optimization_barrier((whole_weight, feature_block))
    projected_rows = jnp.dot(token_rows, whole_weight, preferred_element_type=jnp.float32)
    positions = (
        row_start + jnp.arange(row_total, dtype=jnp.int32) + roll_offsets[0]
    ) % stream_length
    cosine_lookup, sine_lookup = rope_tables(positions)
    key_value_rotated = jnp.concatenate(
        [
            apply_rotary(
                projected_rows[:, :key_span_width], cosine_lookup, sine_lookup, KEY_VALUE_HEADS, 1.0
            ),
            projected_rows[:, key_span_width:],
        ],
        axis=1,
    ).astype(jnp.bfloat16)
    query_rot = apply_rotary(
        query_rows.astype(jnp.float32), cosine_lookup, sine_lookup, QUERY_HEADS, 1.0
    ).astype(jnp.bfloat16)
    edge_rows = from_behind(key_value_rotated, SEQ_AXES, 1)
    keys_all = jnp.concatenate([edge_rows, key_value_rotated], axis=0)
    attended, query_diff, grad_all = band_attention(
        query_rot, keys_all, grad_rows, sink_logit_values, row_start
    )
    incoming = from_behind(grad_all[:WINDOW].astype(jnp.bfloat16), SEQ_AXES, -1).astype(
        jnp.float32
    )
    local_gradient = grad_all[WINDOW:]
    local_gradient = jnp.concatenate(
        [local_gradient[: row_total - WINDOW], local_gradient + incoming], axis=0
    )
    query_back = apply_rotary(query_diff, cosine_lookup, sine_lookup, QUERY_HEADS, -1.0).astype(
        jnp.bfloat16
    )
    key_value_backward = jnp.concatenate(
        [
            apply_rotary(
                local_gradient[:, :key_span_width],
                cosine_lookup,
                sine_lookup,
                KEY_VALUE_HEADS,
                -1.0,
            ),
            local_gradient[:, key_span_width:],
        ],
        axis=1,
    ).astype(jnp.bfloat16)
    token_back = lax.dot_general(
        key_value_backward,
        whole_weight,
        (((1,), (1,)), ((), ())),
        preferred_element_type=jnp.float32,
    ).astype(jnp.bfloat16)
    block_term = lax.dot_general(
        feature_block,
        gather_by_exchange(gather_by_exchange(key_value_backward, SEQ_AXES[1:]), SEQ_AXES[:1]),
        (((0,), (0,)), ((), ())),
        preferred_element_type=jnp.float32,
    )
    fsdp_count = lax.axis_size(FSDP_AXES)
    share = block_term.reshape(fsdp_count, -1, 128)
    share = lax.all_to_all(share, FSDP_AXES, split_axis=0, concat_axis=0, tiled=True)
    weight_share = jnp.sum(share, axis=0)
    return (attended[None], query_back[None], token_back[None], weight_share[None])


def solution(mesh):
    fsdp_count = mesh.shape["fsdp"]
    seq_count = mesh.shape["seq"]
    split_mesh = jax.sharding.Mesh(
        mesh.devices.reshape(fsdp_count // 4, 2, 2, 2, seq_count // 2), FSDP_AXES + SEQ_AXES
    )
    placed = (
        P(FSDP_AXES, SEQ_AXES, None),
        P(FSDP_AXES, SEQ_AXES, None),
        P(FSDP_AXES, None),
        P(),
        P(FSDP_AXES),
        P(FSDP_AXES, SEQ_AXES, None),
    )
    return jax.shard_map(
        local,
        mesh=split_mesh,
        in_specs=placed,
        out_specs=(
            P(FSDP_AXES, SEQ_AXES, None),
            P(FSDP_AXES, SEQ_AXES, None),
            P(FSDP_AXES, SEQ_AXES, None),
            P(SEQ_AXES, FSDP_AXES, None),
        ),
        check_vma=False,
    )
```

```python
import jax
import jax.numpy as jnp
from jax import lax
from jax.experimental import pallas as pl
from jax.experimental.pallas import tpu as pltpu
from jax.sharding import PartitionSpec as P

QUERY_HEADS = 32
KEY_VALUE_HEADS = 4
HEAD_SIZE = 64
WINDOW = 128


rope_base = 150000.0


def from_behind(array, axis, by):
    peers = lax.axis_size(axis)
    pairs = [(i, i + by) for i in range(peers) if 0 <= i + by < peers]
    return lax.ppermute(array, axis, pairs)


def rope_tables(positions):
    half_width = HEAD_SIZE // 2
    frequency = rope_base ** (-jnp.arange(half_width, dtype=jnp.float32) / half_width)
    angle = positions.astype(jnp.float32)[:, None] * frequency[None, :]
    return (jnp.cos(angle), jnp.sin(angle))


def apply_rotary(values, cosine_lookup, sine_lookup, head_count, direction):
    row_count = values.shape[0]
    halves = values.reshape(row_count, head_count, 2, HEAD_SIZE // 2)
    front_half = halves[:, :, 0]
    back_half = halves[:, :, 1]
    cosine_rows = cosine_lookup[:, None, :]
    sine_rows = sine_lookup[:, None, :] * direction
    turned = jnp.stack(
        [
            front_half * cosine_rows - back_half * sine_rows,
            front_half * sine_rows + back_half * cosine_rows,
        ],
        axis=2,
    )
    return turned.reshape(row_count, head_count * HEAD_SIZE)


def band_kernel(sink_ref, lead_ref, q_ref, g_ref, k_ref, v_ref, attn_ref, dq_ref, dk_ref, dv_ref):
    score_scale = HEAD_SIZE ** (-0.5)
    group_width = QUERY_HEADS // KEY_VALUE_HEADS
    row_count = q_ref.shape[1]
    key_count = k_ref.shape[1]
    rows = lax.broadcasted_iota(jnp.int32, (row_count, key_count), 0)
    cols = lax.broadcasted_iota(jnp.int32, (row_count, key_count), 1)
    allowed = (cols > rows) & (cols <= rows + WINDOW) & (cols >= lead_ref[0])
    trans_a = (((0,), (0,)), ((), ()))
    trans_b = (((1,), (1,)), ((), ()))
    for group in range(KEY_VALUE_HEADS):
        key_g = k_ref[group]
        value_g = v_ref[group]

        def head_step(member, carry):
            key_acc, value_acc = carry
            head = group * group_width + member
            query_h = q_ref[head]
            grad_h = g_ref[head]
            scores = (
                lax.dot_general(query_h, key_g, trans_b, preferred_element_type=jnp.float32)
                * score_scale
            )
            exponent = jnp.where(allowed, jnp.exp(scores), 0.0)
            denominator = sink_ref[head] + jnp.sum(exponent, axis=1, keepdims=True)
            softmax_w = exponent / denominator
            softmax_b = softmax_w.astype(jnp.bfloat16)
            attn_ref[head] = jnp.dot(
                softmax_b, value_g, preferred_element_type=jnp.float32
            ).astype(jnp.bfloat16)
            dprob = lax.dot_general(grad_h, value_g, trans_b, preferred_element_type=jnp.float32)
            row_delta = jnp.sum(softmax_w * dprob, axis=1, keepdims=True)
            dscore = (softmax_w * (dprob - row_delta) * score_scale).astype(jnp.bfloat16)
            dq_ref[head] = jnp.dot(dscore, key_g, preferred_element_type=jnp.float32)
            key_acc = key_acc + lax.dot_general(
                dscore, query_h, trans_a, preferred_element_type=jnp.float32
            )
            value_acc = value_acc + lax.dot_general(
                softmax_b, grad_h, trans_a, preferred_element_type=jnp.float32
            )
            return key_acc, value_acc

        start = jnp.zeros((key_count, HEAD_SIZE), jnp.float32)
        key_acc, value_acc = lax.fori_loop(
            0, group_width, head_step, (start, start), unroll=True
        )
        dk_ref[group] = key_acc
        dv_ref[group] = value_acc


def band_attention(query_rot, keys_all, grad_out, sink_logit_values, row_start):
    row_total = query_rot.shape[0]
    key_total = keys_all.shape[0]
    key_span_width = KEY_VALUE_HEADS * HEAD_SIZE
    q_heads = query_rot.reshape(row_total, QUERY_HEADS, HEAD_SIZE).transpose(1, 0, 2)
    g_heads = grad_out.reshape(row_total, QUERY_HEADS, HEAD_SIZE).transpose(1, 0, 2)
    k_heads = (
        keys_all[:, :key_span_width].reshape(key_total, KEY_VALUE_HEADS, HEAD_SIZE).transpose(1, 0, 2)
    )
    v_heads = (
        keys_all[:, key_span_width:].reshape(key_total, KEY_VALUE_HEADS, HEAD_SIZE).transpose(1, 0, 2)
    )
    sink_weight = jnp.exp(sink_logit_values)
    lead = jnp.maximum(WINDOW - row_start, 0).astype(jnp.int32).reshape(1)
    smem = pl.BlockSpec(memory_space=pltpu.SMEM)
    vmem = pl.BlockSpec(memory_space=pltpu.VMEM)
    attn_h, dq_h, dk_h, dv_h = pl.pallas_call(
        band_kernel,
        out_shape=(
            jax.ShapeDtypeStruct(q_heads.shape, jnp.bfloat16),
            jax.ShapeDtypeStruct(q_heads.shape, jnp.float32),
            jax.ShapeDtypeStruct(k_heads.shape, jnp.float32),
            jax.ShapeDtypeStruct(k_heads.shape, jnp.float32),
        ),
        in_specs=[smem, smem, vmem, vmem, vmem, vmem],
        out_specs=(vmem, vmem, vmem, vmem),
    )(sink_weight, lead, q_heads, g_heads, k_heads, v_heads)
    attended = attn_h.transpose(1, 0, 2).reshape(row_total, QUERY_HEADS * HEAD_SIZE)
    query_diff = dq_h.transpose(1, 0, 2).reshape(row_total, QUERY_HEADS * HEAD_SIZE)
    kv_diff = jnp.concatenate(
        [
            dk_h.transpose(1, 0, 2).reshape(key_total, key_span_width),
            dv_h.transpose(1, 0, 2).reshape(key_total, key_span_width),
        ],
        axis=1,
    )
    return attended, query_diff, kv_diff


FSDP_AXES = ("z", "xl", "c")
SEQ_AXES = ("xh", "y")


def gather_by_exchange(array, axes):
    peers = lax.axis_size(axes)
    copies = jnp.broadcast_to(array[None], (peers,) + array.shape)
    copies = lax.all_to_all(copies, axes, split_axis=0, concat_axis=0, tiled=True)
    return copies.reshape(peers * array.shape[0], *array.shape[1:])


def gather_pair(array, axis):
    other = lax.ppermute(array, axis, [(0, 1), (1, 0)])
    first = lax.axis_index(axis) == 0
    return jnp.concatenate(
        [jnp.where(first, array, other), jnp.where(first, other, array)], axis=0
    )


def local(tokens, queries, kv_weight, sink_logit_values, roll_offsets, out_grad):
    token_rows = tokens[0]
    query_rows = queries[0]
    grad_rows = out_grad[0]
    row_total = token_rows.shape[0]
    key_span_width = KEY_VALUE_HEADS * HEAD_SIZE
    seq_index = lax.axis_index(SEQ_AXES)
    seq_count = lax.axis_size(SEQ_AXES)
    stream_length = row_total * seq_count
    row_start = seq_index * row_total
    whole_weight = kv_weight
    for axis in reversed(FSDP_AXES):
        whole_weight = lax.all_gather(whole_weight, axis, axis=0, tiled=True)
    feature_block = lax.all_to_all(token_rows, SEQ_AXES, split_axis=1, concat_axis=0, tiled=True)
    whole_weight, feature_block = lax.optimization_barrier((whole_weight, feature_block))
    projected_rows = jnp.dot(token_rows, whole_weight, preferred_element_type=jnp.float32)
    positions = (
        row_start + jnp.arange(row_total, dtype=jnp.int32) + roll_offsets[0]
    ) % stream_length
    cosine_lookup, sine_lookup = rope_tables(positions)
    key_value_rotated = jnp.concatenate(
        [
            apply_rotary(
                projected_rows[:, :key_span_width], cosine_lookup, sine_lookup, KEY_VALUE_HEADS, 1.0
            ),
            projected_rows[:, key_span_width:],
        ],
        axis=1,
    ).astype(jnp.bfloat16)
    query_rot = apply_rotary(
        query_rows.astype(jnp.float32), cosine_lookup, sine_lookup, QUERY_HEADS, 1.0
    ).astype(jnp.bfloat16)
    edge_rows = from_behind(key_value_rotated, SEQ_AXES, 1)
    keys_all = jnp.concatenate([edge_rows, key_value_rotated], axis=0)
    attended, query_diff, grad_all = band_attention(
        query_rot, keys_all, grad_rows, sink_logit_values, row_start
    )
    incoming = from_behind(grad_all[:WINDOW].astype(jnp.bfloat16), SEQ_AXES, -1).astype(
        jnp.float32
    )
    local_gradient = grad_all[WINDOW:]
    local_gradient = jnp.concatenate(
        [local_gradient[: row_total - WINDOW], local_gradient + incoming], axis=0
    )
    query_back = apply_rotary(query_diff, cosine_lookup, sine_lookup, QUERY_HEADS, -1.0).astype(
        jnp.bfloat16
    )
    key_value_backward = jnp.concatenate(
        [
            apply_rotary(
                local_gradient[:, :key_span_width],
                cosine_lookup,
                sine_lookup,
                KEY_VALUE_HEADS,
                -1.0,
            ),
            local_gradient[:, key_span_width:],
        ],
        axis=1,
    ).astype(jnp.bfloat16)
    token_back = lax.dot_general(
        key_value_backward,
        whole_weight,
        (((1,), (1,)), ((), ())),
        preferred_element_type=jnp.float32,
    ).astype(jnp.bfloat16)
    block_term = lax.dot_general(
        feature_block,
        gather_pair(gather_by_exchange(key_value_backward, SEQ_AXES[1:]), SEQ_AXES[0]),
        (((0,), (0,)), ((), ())),
        preferred_element_type=jnp.float32,
    )
    fsdp_count = lax.axis_size(FSDP_AXES)
    share = block_term.reshape(fsdp_count, -1, 128)
    share = lax.all_to_all(share, FSDP_AXES, split_axis=0, concat_axis=0, tiled=True)
    weight_share = jnp.sum(share, axis=0)
    return (attended[None], query_back[None], token_back[None], weight_share[None])


def solution(mesh):
    fsdp_count = mesh.shape["fsdp"]
    seq_count = mesh.shape["seq"]
    split_mesh = jax.sharding.Mesh(
        mesh.devices.reshape(fsdp_count // 4, 2, 2, 2, seq_count // 2), FSDP_AXES + SEQ_AXES
    )
    placed = (
        P(FSDP_AXES, SEQ_AXES, None),
        P(FSDP_AXES, SEQ_AXES, None),
        P(FSDP_AXES, None),
        P(),
        P(FSDP_AXES),
        P(FSDP_AXES, SEQ_AXES, None),
    )
    return jax.shard_map(
        local,
        mesh=split_mesh,
        in_specs=placed,
        out_specs=(
            P(FSDP_AXES, SEQ_AXES, None),
            P(FSDP_AXES, SEQ_AXES, None),
            P(FSDP_AXES, SEQ_AXES, None),
            P(SEQ_AXES, FSDP_AXES, None),
        ),
        check_vma=False,
    )
```

```python
import jax
import jax.numpy as jnp
from jax import lax
from jax.experimental import pallas as pl
from jax.experimental.pallas import tpu as pltpu
from jax.sharding import PartitionSpec as P

QUERY_HEADS = 32
KEY_VALUE_HEADS = 4
HEAD_SIZE = 64
WINDOW = 128


rope_base = 150000.0


def from_behind(array, axis, by):
    peers = lax.axis_size(axis)
    pairs = [(i, i + by) for i in range(peers) if 0 <= i + by < peers]
    return lax.ppermute(array, axis, pairs)


def rope_tables(positions):
    half_width = HEAD_SIZE // 2
    frequency = rope_base ** (-jnp.arange(half_width, dtype=jnp.float32) / half_width)
    angle = positions.astype(jnp.float32)[:, None] * frequency[None, :]
    return (jnp.cos(angle), jnp.sin(angle))


def apply_rotary(values, cosine_lookup, sine_lookup, head_count, direction):
    row_count = values.shape[0]
    halves = values.reshape(row_count, head_count, 2, HEAD_SIZE // 2)
    front_half = halves[:, :, 0]
    back_half = halves[:, :, 1]
    cosine_rows = cosine_lookup[:, None, :]
    sine_rows = sine_lookup[:, None, :] * direction
    turned = jnp.stack(
        [
            front_half * cosine_rows - back_half * sine_rows,
            front_half * sine_rows + back_half * cosine_rows,
        ],
        axis=2,
    )
    return turned.reshape(row_count, head_count * HEAD_SIZE)


def band_kernel(sink_ref, lead_ref, q_ref, g_ref, k_ref, v_ref, attn_ref, dq_ref, dk_ref, dv_ref):
    score_scale = HEAD_SIZE ** (-0.5)
    group_width = QUERY_HEADS // KEY_VALUE_HEADS
    row_count = q_ref.shape[1]
    key_count = k_ref.shape[1]
    rows = lax.broadcasted_iota(jnp.int32, (row_count, key_count), 0)
    cols = lax.broadcasted_iota(jnp.int32, (row_count, key_count), 1)
    allowed = (cols > rows) & (cols <= rows + WINDOW) & (cols >= lead_ref[0])
    trans_a = (((0,), (0,)), ((), ()))
    trans_b = (((1,), (1,)), ((), ()))
    for group in range(KEY_VALUE_HEADS):
        key_g = k_ref[group]
        value_g = v_ref[group]

        def head_step(member, carry):
            key_acc, value_acc = carry
            head = group * group_width + member
            query_h = q_ref[head]
            grad_h = g_ref[head]
            scores = (
                lax.dot_general(query_h, key_g, trans_b, preferred_element_type=jnp.float32)
                * score_scale
            )
            exponent = jnp.where(allowed, jnp.exp(scores), 0.0)
            denominator = sink_ref[head] + jnp.sum(exponent, axis=1, keepdims=True)
            softmax_w = exponent / denominator
            softmax_b = softmax_w.astype(jnp.bfloat16)
            attn_ref[head] = jnp.dot(
                softmax_b, value_g, preferred_element_type=jnp.float32
            ).astype(jnp.bfloat16)
            dprob = lax.dot_general(grad_h, value_g, trans_b, preferred_element_type=jnp.float32)
            row_delta = jnp.sum(softmax_w * dprob, axis=1, keepdims=True)
            dscore = (softmax_w * (dprob - row_delta) * score_scale).astype(jnp.bfloat16)
            dq_ref[head] = jnp.dot(dscore, key_g, preferred_element_type=jnp.float32)
            key_acc = key_acc + lax.dot_general(
                dscore, query_h, trans_a, preferred_element_type=jnp.float32
            )
            value_acc = value_acc + lax.dot_general(
                softmax_b, grad_h, trans_a, preferred_element_type=jnp.float32
            )
            return key_acc, value_acc

        start = jnp.zeros((key_count, HEAD_SIZE), jnp.float32)
        key_acc, value_acc = lax.fori_loop(
            0, group_width, head_step, (start, start), unroll=True
        )
        dk_ref[group] = key_acc
        dv_ref[group] = value_acc


def band_attention(query_rot, keys_all, grad_out, sink_logit_values, row_start):
    row_total = query_rot.shape[0]
    key_total = keys_all.shape[0]
    key_span_width = KEY_VALUE_HEADS * HEAD_SIZE
    q_heads = query_rot.reshape(row_total, QUERY_HEADS, HEAD_SIZE).transpose(1, 0, 2)
    g_heads = grad_out.reshape(row_total, QUERY_HEADS, HEAD_SIZE).transpose(1, 0, 2)
    k_heads = (
        keys_all[:, :key_span_width].reshape(key_total, KEY_VALUE_HEADS, HEAD_SIZE).transpose(1, 0, 2)
    )
    v_heads = (
        keys_all[:, key_span_width:].reshape(key_total, KEY_VALUE_HEADS, HEAD_SIZE).transpose(1, 0, 2)
    )
    sink_weight = jnp.exp(sink_logit_values)
    lead = jnp.maximum(WINDOW - row_start, 0).astype(jnp.int32).reshape(1)
    smem = pl.BlockSpec(memory_space=pltpu.SMEM)
    vmem = pl.BlockSpec(memory_space=pltpu.VMEM)
    attn_h, dq_h, dk_h, dv_h = pl.pallas_call(
        band_kernel,
        out_shape=(
            jax.ShapeDtypeStruct(q_heads.shape, jnp.bfloat16),
            jax.ShapeDtypeStruct(q_heads.shape, jnp.float32),
            jax.ShapeDtypeStruct(k_heads.shape, jnp.float32),
            jax.ShapeDtypeStruct(k_heads.shape, jnp.float32),
        ),
        in_specs=[smem, smem, vmem, vmem, vmem, vmem],
        out_specs=(vmem, vmem, vmem, vmem),
    )(sink_weight, lead, q_heads, g_heads, k_heads, v_heads)
    attended = attn_h.transpose(1, 0, 2).reshape(row_total, QUERY_HEADS * HEAD_SIZE)
    query_diff = dq_h.transpose(1, 0, 2).reshape(row_total, QUERY_HEADS * HEAD_SIZE)
    kv_diff = jnp.concatenate(
        [
            dk_h.transpose(1, 0, 2).reshape(key_total, key_span_width),
            dv_h.transpose(1, 0, 2).reshape(key_total, key_span_width),
        ],
        axis=1,
    )
    return attended, query_diff, kv_diff


FSDP_AXES = ("z", "xl", "c")
SEQ_AXES = ("xh", "y")


def gather_by_exchange(array, axes):
    peers = lax.axis_size(axes)
    copies = jnp.broadcast_to(array[None], (peers,) + array.shape)
    copies = lax.all_to_all(copies, axes, split_axis=0, concat_axis=0, tiled=True)
    return copies.reshape(peers * array.shape[0], *array.shape[1:])


def gather_pair(array, axis):
    other = lax.ppermute(array, axis, [(0, 1), (1, 0)])
    first = lax.axis_index(axis) == 0
    return jnp.concatenate(
        [jnp.where(first, array, other), jnp.where(first, other, array)], axis=0
    )


def local(tokens, queries, kv_weight, sink_logit_values, roll_offsets, out_grad):
    token_rows = tokens[0]
    query_rows = queries[0]
    grad_rows = out_grad[0]
    row_total = token_rows.shape[0]
    key_span_width = KEY_VALUE_HEADS * HEAD_SIZE
    seq_index = lax.axis_index(SEQ_AXES)
    seq_count = lax.axis_size(SEQ_AXES)
    stream_length = row_total * seq_count
    row_start = seq_index * row_total
    whole_weight = kv_weight
    for axis in reversed(FSDP_AXES[1:]):
        whole_weight = lax.all_gather(whole_weight, axis, axis=0, tiled=True)
    half_width = whole_weight.shape[1] // 2
    first_core = lax.axis_index(FSDP_AXES[2]) == 0
    own_half = jnp.where(first_core, whole_weight[:, :half_width], whole_weight[:, half_width:])
    own_half = lax.all_gather(own_half, FSDP_AXES[0], axis=0, tiled=True)
    feature_block = lax.all_to_all(token_rows, SEQ_AXES, split_axis=1, concat_axis=0, tiled=True)
    own_half, feature_block = lax.optimization_barrier((own_half, feature_block))
    other_half = lax.ppermute(own_half, FSDP_AXES[2], [(0, 1), (1, 0)])
    whole_weight = jnp.where(
        first_core,
        jnp.concatenate([own_half, other_half], axis=1),
        jnp.concatenate([other_half, own_half], axis=1),
    )
    projected_rows = jnp.dot(token_rows, whole_weight, preferred_element_type=jnp.float32)
    positions = (
        row_start + jnp.arange(row_total, dtype=jnp.int32) + roll_offsets[0]
    ) % stream_length
    cosine_lookup, sine_lookup = rope_tables(positions)
    key_value_rotated = jnp.concatenate(
        [
            apply_rotary(
                projected_rows[:, :key_span_width], cosine_lookup, sine_lookup, KEY_VALUE_HEADS, 1.0
            ),
            projected_rows[:, key_span_width:],
        ],
        axis=1,
    ).astype(jnp.bfloat16)
    query_rot = apply_rotary(
        query_rows.astype(jnp.float32), cosine_lookup, sine_lookup, QUERY_HEADS, 1.0
    ).astype(jnp.bfloat16)
    edge_rows = from_behind(key_value_rotated, SEQ_AXES, 1)
    keys_all = jnp.concatenate([edge_rows, key_value_rotated], axis=0)
    attended, query_diff, grad_all = band_attention(
        query_rot, keys_all, grad_rows, sink_logit_values, row_start
    )
    incoming = from_behind(grad_all[:WINDOW].astype(jnp.bfloat16), SEQ_AXES, -1).astype(
        jnp.float32
    )
    local_gradient = grad_all[WINDOW:]
    local_gradient = jnp.concatenate(
        [local_gradient[: row_total - WINDOW], local_gradient + incoming], axis=0
    )
    query_back = apply_rotary(query_diff, cosine_lookup, sine_lookup, QUERY_HEADS, -1.0).astype(
        jnp.bfloat16
    )
    key_value_backward = jnp.concatenate(
        [
            apply_rotary(
                local_gradient[:, :key_span_width],
                cosine_lookup,
                sine_lookup,
                KEY_VALUE_HEADS,
                -1.0,
            ),
            local_gradient[:, key_span_width:],
        ],
        axis=1,
    ).astype(jnp.bfloat16)
    token_back = lax.dot_general(
        key_value_backward,
        whole_weight,
        (((1,), (1,)), ((), ())),
        preferred_element_type=jnp.float32,
    ).astype(jnp.bfloat16)
    block_term = lax.dot_general(
        feature_block,
        gather_pair(gather_by_exchange(key_value_backward, SEQ_AXES[1:]), SEQ_AXES[0]),
        (((0,), (0,)), ((), ())),
        preferred_element_type=jnp.float32,
    )
    fsdp_count = lax.axis_size(FSDP_AXES)
    share = block_term.reshape(fsdp_count, -1, 128)
    share = lax.all_to_all(share, FSDP_AXES, split_axis=0, concat_axis=0, tiled=True)
    weight_share = jnp.sum(share, axis=0)
    return (attended[None], query_back[None], token_back[None], weight_share[None])


def solution(mesh):
    fsdp_count = mesh.shape["fsdp"]
    seq_count = mesh.shape["seq"]
    split_mesh = jax.sharding.Mesh(
        mesh.devices.reshape(fsdp_count // 4, 2, 2, 2, seq_count // 2), FSDP_AXES + SEQ_AXES
    )
    placed = (
        P(FSDP_AXES, SEQ_AXES, None),
        P(FSDP_AXES, SEQ_AXES, None),
        P(FSDP_AXES, None),
        P(),
        P(FSDP_AXES),
        P(FSDP_AXES, SEQ_AXES, None),
    )
    return jax.shard_map(
        local,
        mesh=split_mesh,
        in_specs=placed,
        out_specs=(
            P(FSDP_AXES, SEQ_AXES, None),
            P(FSDP_AXES, SEQ_AXES, None),
            P(FSDP_AXES, SEQ_AXES, None),
            P(SEQ_AXES, FSDP_AXES, None),
        ),
        check_vma=False,
    )
```

```python
import jax
import jax.numpy as jnp
from jax import lax
from jax.experimental import pallas as pl
from jax.experimental.pallas import tpu as pltpu
from jax.sharding import PartitionSpec as P

QUERY_HEADS = 32
KEY_VALUE_HEADS = 4
HEAD_SIZE = 64
WINDOW = 128


rope_base = 150000.0


def from_behind(array, axis, by):
    peers = lax.axis_size(axis)
    pairs = [(i, i + by) for i in range(peers) if 0 <= i + by < peers]
    return lax.ppermute(array, axis, pairs)


def rope_tables(positions):
    half_width = HEAD_SIZE // 2
    frequency = rope_base ** (-jnp.arange(half_width, dtype=jnp.float32) / half_width)
    angle = positions.astype(jnp.float32)[:, None] * frequency[None, :]
    return (jnp.cos(angle), jnp.sin(angle))


def apply_rotary(values, cosine_lookup, sine_lookup, head_count, direction):
    row_count = values.shape[0]
    halves = values.reshape(row_count, head_count, 2, HEAD_SIZE // 2)
    front_half = halves[:, :, 0]
    back_half = halves[:, :, 1]
    cosine_rows = cosine_lookup[:, None, :]
    sine_rows = sine_lookup[:, None, :] * direction
    turned = jnp.stack(
        [
            front_half * cosine_rows - back_half * sine_rows,
            front_half * sine_rows + back_half * cosine_rows,
        ],
        axis=2,
    )
    return turned.reshape(row_count, head_count * HEAD_SIZE)


def band_kernel(sink_ref, lead_ref, q_ref, g_ref, k_ref, v_ref, attn_ref, dq_ref, dk_ref, dv_ref):
    score_scale = HEAD_SIZE ** (-0.5)
    group_width = QUERY_HEADS // KEY_VALUE_HEADS
    row_count = q_ref.shape[1]
    key_count = k_ref.shape[1]
    rows = lax.broadcasted_iota(jnp.int32, (row_count, key_count), 0)
    cols = lax.broadcasted_iota(jnp.int32, (row_count, key_count), 1)
    allowed = (cols > rows) & (cols <= rows + WINDOW) & (cols >= lead_ref[0])
    trans_a = (((0,), (0,)), ((), ()))
    trans_b = (((1,), (1,)), ((), ()))
    for group in range(KEY_VALUE_HEADS):
        key_g = k_ref[group]
        value_g = v_ref[group]

        def head_step(member, carry):
            key_acc, value_acc = carry
            head = group * group_width + member
            query_h = q_ref[head]
            grad_h = g_ref[head]
            scores = (
                lax.dot_general(query_h, key_g, trans_b, preferred_element_type=jnp.float32)
                * score_scale
            )
            exponent = jnp.where(allowed, jnp.exp(scores), 0.0)
            denominator = sink_ref[head] + jnp.sum(exponent, axis=1, keepdims=True)
            softmax_w = exponent / denominator
            softmax_b = softmax_w.astype(jnp.bfloat16)
            attn_ref[head] = jnp.dot(
                softmax_b, value_g, preferred_element_type=jnp.float32
            ).astype(jnp.bfloat16)
            dprob = lax.dot_general(grad_h, value_g, trans_b, preferred_element_type=jnp.float32)
            row_delta = jnp.sum(softmax_w * dprob, axis=1, keepdims=True)
            dscore = (softmax_w * (dprob - row_delta) * score_scale).astype(jnp.bfloat16)
            dq_ref[head] = jnp.dot(dscore, key_g, preferred_element_type=jnp.float32)
            key_acc = key_acc + lax.dot_general(
                dscore, query_h, trans_a, preferred_element_type=jnp.float32
            )
            value_acc = value_acc + lax.dot_general(
                softmax_b, grad_h, trans_a, preferred_element_type=jnp.float32
            )
            return key_acc, value_acc

        start = jnp.zeros((key_count, HEAD_SIZE), jnp.float32)
        key_acc, value_acc = lax.fori_loop(
            0, group_width, head_step, (start, start), unroll=True
        )
        dk_ref[group] = key_acc
        dv_ref[group] = value_acc


def band_attention(query_rot, keys_all, grad_out, sink_logit_values, row_start):
    row_total = query_rot.shape[0]
    key_total = keys_all.shape[0]
    key_span_width = KEY_VALUE_HEADS * HEAD_SIZE
    q_heads = query_rot.reshape(row_total, QUERY_HEADS, HEAD_SIZE).transpose(1, 0, 2)
    g_heads = grad_out.reshape(row_total, QUERY_HEADS, HEAD_SIZE).transpose(1, 0, 2)
    k_heads = (
        keys_all[:, :key_span_width].reshape(key_total, KEY_VALUE_HEADS, HEAD_SIZE).transpose(1, 0, 2)
    )
    v_heads = (
        keys_all[:, key_span_width:].reshape(key_total, KEY_VALUE_HEADS, HEAD_SIZE).transpose(1, 0, 2)
    )
    sink_weight = jnp.exp(sink_logit_values)
    lead = jnp.maximum(WINDOW - row_start, 0).astype(jnp.int32).reshape(1)
    smem = pl.BlockSpec(memory_space=pltpu.SMEM)
    vmem = pl.BlockSpec(memory_space=pltpu.VMEM)
    attn_h, dq_h, dk_h, dv_h = pl.pallas_call(
        band_kernel,
        out_shape=(
            jax.ShapeDtypeStruct(q_heads.shape, jnp.bfloat16),
            jax.ShapeDtypeStruct(q_heads.shape, jnp.float32),
            jax.ShapeDtypeStruct(k_heads.shape, jnp.float32),
            jax.ShapeDtypeStruct(k_heads.shape, jnp.float32),
        ),
        in_specs=[smem, smem, vmem, vmem, vmem, vmem],
        out_specs=(vmem, vmem, vmem, vmem),
    )(sink_weight, lead, q_heads, g_heads, k_heads, v_heads)
    attended = attn_h.transpose(1, 0, 2).reshape(row_total, QUERY_HEADS * HEAD_SIZE)
    query_diff = dq_h.transpose(1, 0, 2).reshape(row_total, QUERY_HEADS * HEAD_SIZE)
    kv_diff = jnp.concatenate(
        [
            dk_h.transpose(1, 0, 2).reshape(key_total, key_span_width),
            dv_h.transpose(1, 0, 2).reshape(key_total, key_span_width),
        ],
        axis=1,
    )
    return attended, query_diff, kv_diff


FSDP_AXES = ("z", "xl", "c")
SEQ_AXES = ("xh", "y")


def gather_by_exchange(array, axes):
    peers = lax.axis_size(axes)
    copies = jnp.broadcast_to(array[None], (peers,) + array.shape)
    copies = lax.all_to_all(copies, axes, split_axis=0, concat_axis=0, tiled=True)
    return copies.reshape(peers * array.shape[0], *array.shape[1:])


def gather_pair(array, axis):
    other = lax.ppermute(array, axis, [(0, 1), (1, 0)])
    first = lax.axis_index(axis) == 0
    return jnp.concatenate(
        [jnp.where(first, array, other), jnp.where(first, other, array)], axis=0
    )


def local(tokens, queries, kv_weight, sink_logit_values, roll_offsets, out_grad):
    token_rows = tokens[0]
    query_rows = queries[0]
    grad_rows = out_grad[0]
    row_total = token_rows.shape[0]
    key_span_width = KEY_VALUE_HEADS * HEAD_SIZE
    seq_index = lax.axis_index(SEQ_AXES)
    seq_count = lax.axis_size(SEQ_AXES)
    stream_length = row_total * seq_count
    row_start = seq_index * row_total
    whole_weight = kv_weight
    for axis in reversed(FSDP_AXES):
        whole_weight = lax.all_gather(whole_weight, axis, axis=0, tiled=True)
    feature_block = lax.all_to_all(token_rows, SEQ_AXES, split_axis=1, concat_axis=0, tiled=True)
    whole_weight, feature_block = lax.optimization_barrier((whole_weight, feature_block))
    projected_rows = jnp.dot(token_rows, whole_weight, preferred_element_type=jnp.float32)
    positions = (
        row_start + jnp.arange(row_total, dtype=jnp.int32) + roll_offsets[0]
    ) % stream_length
    cosine_lookup, sine_lookup = rope_tables(positions)
    key_value_rotated = jnp.concatenate(
        [
            apply_rotary(
                projected_rows[:, :key_span_width], cosine_lookup, sine_lookup, KEY_VALUE_HEADS, 1.0
            ),
            projected_rows[:, key_span_width:],
        ],
        axis=1,
    ).astype(jnp.bfloat16)
    query_rot = apply_rotary(
        query_rows.astype(jnp.float32), cosine_lookup, sine_lookup, QUERY_HEADS, 1.0
    ).astype(jnp.bfloat16)
    edge_rows = from_behind(key_value_rotated, SEQ_AXES, 1)
    keys_all = jnp.concatenate([edge_rows, key_value_rotated], axis=0)
    attended, query_diff, grad_all = band_attention(
        query_rot, keys_all, grad_rows, sink_logit_values, row_start
    )
    incoming = from_behind(grad_all[:WINDOW].astype(jnp.bfloat16), SEQ_AXES, -1).astype(
        jnp.float32
    )
    local_gradient = grad_all[WINDOW:]
    local_gradient = jnp.concatenate(
        [local_gradient[: row_total - WINDOW], local_gradient + incoming], axis=0
    )
    query_back = apply_rotary(query_diff, cosine_lookup, sine_lookup, QUERY_HEADS, -1.0).astype(
        jnp.bfloat16
    )
    key_value_backward = jnp.concatenate(
        [
            apply_rotary(
                local_gradient[:, :key_span_width],
                cosine_lookup,
                sine_lookup,
                KEY_VALUE_HEADS,
                -1.0,
            ),
            local_gradient[:, key_span_width:],
        ],
        axis=1,
    ).astype(jnp.bfloat16)
    token_back = lax.dot_general(
        key_value_backward,
        whole_weight,
        (((1,), (1,)), ((), ())),
        preferred_element_type=jnp.float32,
    ).astype(jnp.bfloat16)
    block_term = lax.dot_general(
        feature_block,
        gather_pair(gather_by_exchange(key_value_backward, SEQ_AXES[1:]), SEQ_AXES[0]),
        (((0,), (0,)), ((), ())),
        preferred_element_type=jnp.float32,
    )
    fsdp_count = lax.axis_size(FSDP_AXES)
    share = block_term.reshape(fsdp_count, -1, 128).astype(jnp.bfloat16)
    share = lax.all_to_all(share, FSDP_AXES, split_axis=0, concat_axis=0, tiled=True)
    weight_share = jnp.sum(share.astype(jnp.float32), axis=0)
    return (attended[None], query_back[None], token_back[None], weight_share[None])


def solution(mesh):
    fsdp_count = mesh.shape["fsdp"]
    seq_count = mesh.shape["seq"]
    split_mesh = jax.sharding.Mesh(
        mesh.devices.reshape(fsdp_count // 4, 2, 2, 2, seq_count // 2), FSDP_AXES + SEQ_AXES
    )
    placed = (
        P(FSDP_AXES, SEQ_AXES, None),
        P(FSDP_AXES, SEQ_AXES, None),
        P(FSDP_AXES, None),
        P(),
        P(FSDP_AXES),
        P(FSDP_AXES, SEQ_AXES, None),
    )
    return jax.shard_map(
        local,
        mesh=split_mesh,
        in_specs=placed,
        out_specs=(
            P(FSDP_AXES, SEQ_AXES, None),
            P(FSDP_AXES, SEQ_AXES, None),
            P(FSDP_AXES, SEQ_AXES, None),
            P(SEQ_AXES, FSDP_AXES, None),
        ),
        check_vma=False,
    )
```

```python
import jax
import jax.numpy as jnp
from jax import lax
from jax.experimental import pallas as pl
from jax.experimental.pallas import tpu as pltpu
from jax.sharding import PartitionSpec as P

QUERY_HEADS = 32
KEY_VALUE_HEADS = 4
HEAD_SIZE = 64
WINDOW = 128


rope_base = 150000.0


def from_behind(array, axis, by):
    peers = lax.axis_size(axis)
    pairs = [(i, i + by) for i in range(peers) if 0 <= i + by < peers]
    return lax.ppermute(array, axis, pairs)


def rope_tables(positions):
    half_width = HEAD_SIZE // 2
    frequency = rope_base ** (-jnp.arange(half_width, dtype=jnp.float32) / half_width)
    angle = positions.astype(jnp.float32)[:, None] * frequency[None, :]
    return (jnp.cos(angle), jnp.sin(angle))


def apply_rotary(values, cosine_lookup, sine_lookup, head_count, direction):
    row_count = values.shape[0]
    halves = values.reshape(row_count, head_count, 2, HEAD_SIZE // 2)
    front_half = halves[:, :, 0]
    back_half = halves[:, :, 1]
    cosine_rows = cosine_lookup[:, None, :]
    sine_rows = sine_lookup[:, None, :] * direction
    turned = jnp.stack(
        [
            front_half * cosine_rows - back_half * sine_rows,
            front_half * sine_rows + back_half * cosine_rows,
        ],
        axis=2,
    )
    return turned.reshape(row_count, head_count * HEAD_SIZE)


def band_kernel(sink_ref, lead_ref, q_ref, g_ref, k_ref, v_ref, attn_ref, dq_ref, dk_ref, dv_ref):
    score_scale = HEAD_SIZE ** (-0.5)
    group_width = QUERY_HEADS // KEY_VALUE_HEADS
    pair_width = 2 * HEAD_SIZE
    row_count = q_ref.shape[0]
    key_count = k_ref.shape[2]
    rows = lax.broadcasted_iota(jnp.int32, (row_count, key_count), 0)
    cols = lax.broadcasted_iota(jnp.int32, (row_count, key_count), 1)
    allowed = (cols > rows) & (cols <= rows + WINDOW) & (cols >= lead_ref[0])
    lanes = lax.broadcasted_iota(jnp.int32, (row_count, pair_width), 1)
    halves = (lanes < HEAD_SIZE, lanes >= HEAD_SIZE)
    trans_a = (((0,), (0,)), ((), ()))
    trans_b = (((1,), (1,)), ((), ()))
    for group in range(KEY_VALUE_HEADS):
        key_acc = jnp.zeros((key_count, pair_width), jnp.float32)
        value_acc = jnp.zeros((key_count, pair_width), jnp.float32)
        for pair in range(group_width // 2):
            col = (group * group_width + 2 * pair) * HEAD_SIZE
            query_p = q_ref[:, col : col + pair_width]
            grad_p = g_ref[:, col : col + pair_width]
            attn_acc = jnp.zeros((row_count, pair_width), jnp.float32)
            dq_acc = jnp.zeros((row_count, pair_width), jnp.float32)
            for side in range(2):
                head = group * group_width + 2 * pair + side
                key_s = k_ref[group, side]
                value_s = v_ref[group, side]
                scores = (
                    lax.dot_general(query_p, key_s, trans_b, preferred_element_type=jnp.float32)
                    * score_scale
                )
                exponent = jnp.where(allowed, jnp.exp(scores), 0.0)
                denominator = sink_ref[head] + jnp.sum(exponent, axis=1, keepdims=True)
                softmax_w = exponent / denominator
                softmax_b = softmax_w.astype(jnp.bfloat16)
                attn_acc = attn_acc + jnp.dot(
                    softmax_b, value_s, preferred_element_type=jnp.float32
                )
                dprob = lax.dot_general(grad_p, value_s, trans_b, preferred_element_type=jnp.float32)
                row_delta = jnp.sum(softmax_w * dprob, axis=1, keepdims=True)
                dscore = (softmax_w * (dprob - row_delta) * score_scale).astype(jnp.bfloat16)
                dq_acc = dq_acc + jnp.dot(dscore, key_s, preferred_element_type=jnp.float32)
                query_h = jnp.where(halves[side], query_p, jnp.zeros_like(query_p))
                grad_h = jnp.where(halves[side], grad_p, jnp.zeros_like(grad_p))
                key_acc = key_acc + lax.dot_general(
                    dscore, query_h, trans_a, preferred_element_type=jnp.float32
                )
                value_acc = value_acc + lax.dot_general(
                    softmax_b, grad_h, trans_a, preferred_element_type=jnp.float32
                )
            attn_ref[:, col : col + pair_width] = attn_acc.astype(jnp.bfloat16)
            dq_ref[:, col : col + pair_width] = dq_acc
        dk_ref[group] = key_acc
        dv_ref[group] = value_acc


def padded_heads(columns, key_total):
    heads = columns.reshape(key_total, KEY_VALUE_HEADS, HEAD_SIZE).transpose(1, 0, 2)
    blank = jnp.zeros_like(heads)
    return jnp.stack(
        [jnp.concatenate([heads, blank], axis=2), jnp.concatenate([blank, heads], axis=2)], axis=1
    )


def band_attention(query_rot, keys_all, grad_out, sink_logit_values, row_start):
    row_total = query_rot.shape[0]
    key_total = keys_all.shape[0]
    key_span_width = KEY_VALUE_HEADS * HEAD_SIZE
    k_pairs = padded_heads(keys_all[:, :key_span_width], key_total)
    v_pairs = padded_heads(keys_all[:, key_span_width:], key_total)
    sink_weight = jnp.exp(sink_logit_values)
    lead = jnp.maximum(WINDOW - row_start, 0).astype(jnp.int32).reshape(1)
    smem = pl.BlockSpec(memory_space=pltpu.SMEM)
    vmem = pl.BlockSpec(memory_space=pltpu.VMEM)
    acc_shape = (KEY_VALUE_HEADS, key_total, 2 * HEAD_SIZE)
    attended, query_diff, dk_pairs, dv_pairs = pl.pallas_call(
        band_kernel,
        out_shape=(
            jax.ShapeDtypeStruct(query_rot.shape, jnp.bfloat16),
            jax.ShapeDtypeStruct(query_rot.shape, jnp.float32),
            jax.ShapeDtypeStruct(acc_shape, jnp.float32),
            jax.ShapeDtypeStruct(acc_shape, jnp.float32),
        ),
        in_specs=[smem, smem, vmem, vmem, vmem, vmem],
        out_specs=(vmem, vmem, vmem, vmem),
    )(sink_weight, lead, query_rot, grad_out, k_pairs, v_pairs)
    dk_h = dk_pairs[:, :, :HEAD_SIZE] + dk_pairs[:, :, HEAD_SIZE:]
    dv_h = dv_pairs[:, :, :HEAD_SIZE] + dv_pairs[:, :, HEAD_SIZE:]
    kv_diff = jnp.concatenate(
        [
            dk_h.transpose(1, 0, 2).reshape(key_total, key_span_width),
            dv_h.transpose(1, 0, 2).reshape(key_total, key_span_width),
        ],
        axis=1,
    )
    return attended, query_diff, kv_diff


FSDP_AXES = ("z", "xl", "c")
SEQ_AXES = ("xh", "y")


def gather_by_exchange(array, axes):
    peers = lax.axis_size(axes)
    copies = jnp.broadcast_to(array[None], (peers,) + array.shape)
    copies = lax.all_to_all(copies, axes, split_axis=0, concat_axis=0, tiled=True)
    return copies.reshape(peers * array.shape[0], *array.shape[1:])


def gather_pair(array, axis):
    other = lax.ppermute(array, axis, [(0, 1), (1, 0)])
    first = lax.axis_index(axis) == 0
    return jnp.concatenate(
        [jnp.where(first, array, other), jnp.where(first, other, array)], axis=0
    )


def local(tokens, queries, kv_weight, sink_logit_values, roll_offsets, out_grad):
    token_rows = tokens[0]
    query_rows = queries[0]
    grad_rows = out_grad[0]
    row_total = token_rows.shape[0]
    key_span_width = KEY_VALUE_HEADS * HEAD_SIZE
    seq_index = lax.axis_index(SEQ_AXES)
    seq_count = lax.axis_size(SEQ_AXES)
    stream_length = row_total * seq_count
    row_start = seq_index * row_total
    whole_weight = kv_weight
    for axis in reversed(FSDP_AXES):
        whole_weight = lax.all_gather(whole_weight, axis, axis=0, tiled=True)
    feature_block = lax.all_to_all(token_rows, SEQ_AXES, split_axis=1, concat_axis=0, tiled=True)
    whole_weight, feature_block = lax.optimization_barrier((whole_weight, feature_block))
    projected_rows = jnp.dot(token_rows, whole_weight, preferred_element_type=jnp.float32)
    positions = (
        row_start + jnp.arange(row_total, dtype=jnp.int32) + roll_offsets[0]
    ) % stream_length
    cosine_lookup, sine_lookup = rope_tables(positions)
    key_value_rotated = jnp.concatenate(
        [
            apply_rotary(
                projected_rows[:, :key_span_width], cosine_lookup, sine_lookup, KEY_VALUE_HEADS, 1.0
            ),
            projected_rows[:, key_span_width:],
        ],
        axis=1,
    ).astype(jnp.bfloat16)
    query_rot = apply_rotary(
        query_rows.astype(jnp.float32), cosine_lookup, sine_lookup, QUERY_HEADS, 1.0
    ).astype(jnp.bfloat16)
    edge_rows = from_behind(key_value_rotated, SEQ_AXES, 1)
    keys_all = jnp.concatenate([edge_rows, key_value_rotated], axis=0)
    attended, query_diff, grad_all = band_attention(
        query_rot, keys_all, grad_rows, sink_logit_values, row_start
    )
    incoming = from_behind(grad_all[:WINDOW].astype(jnp.bfloat16), SEQ_AXES, -1).astype(
        jnp.float32
    )
    local_gradient = grad_all[WINDOW:]
    local_gradient = jnp.concatenate(
        [local_gradient[: row_total - WINDOW], local_gradient + incoming], axis=0
    )
    query_back = apply_rotary(query_diff, cosine_lookup, sine_lookup, QUERY_HEADS, -1.0).astype(
        jnp.bfloat16
    )
    key_value_backward = jnp.concatenate(
        [
            apply_rotary(
                local_gradient[:, :key_span_width],
                cosine_lookup,
                sine_lookup,
                KEY_VALUE_HEADS,
                -1.0,
            ),
            local_gradient[:, key_span_width:],
        ],
        axis=1,
    ).astype(jnp.bfloat16)
    token_back = lax.dot_general(
        key_value_backward,
        whole_weight,
        (((1,), (1,)), ((), ())),
        preferred_element_type=jnp.float32,
    ).astype(jnp.bfloat16)
    block_term = lax.dot_general(
        feature_block,
        gather_pair(gather_by_exchange(key_value_backward, SEQ_AXES[1:]), SEQ_AXES[0]),
        (((0,), (0,)), ((), ())),
        preferred_element_type=jnp.float32,
    )
    fsdp_count = lax.axis_size(FSDP_AXES)
    share = block_term.reshape(fsdp_count, -1, 128).astype(jnp.bfloat16)
    share = lax.all_to_all(share, FSDP_AXES, split_axis=0, concat_axis=0, tiled=True)
    weight_share = jnp.sum(share.astype(jnp.float32), axis=0)
    return (attended[None], query_back[None], token_back[None], weight_share[None])


def solution(mesh):
    fsdp_count = mesh.shape["fsdp"]
    seq_count = mesh.shape["seq"]
    split_mesh = jax.sharding.Mesh(
        mesh.devices.reshape(fsdp_count // 4, 2, 2, 2, seq_count // 2), FSDP_AXES + SEQ_AXES
    )
    placed = (
        P(FSDP_AXES, SEQ_AXES, None),
        P(FSDP_AXES, SEQ_AXES, None),
        P(FSDP_AXES, None),
        P(),
        P(FSDP_AXES),
        P(FSDP_AXES, SEQ_AXES, None),
    )
    return jax.shard_map(
        local,
        mesh=split_mesh,
        in_specs=placed,
        out_specs=(
            P(FSDP_AXES, SEQ_AXES, None),
            P(FSDP_AXES, SEQ_AXES, None),
            P(FSDP_AXES, SEQ_AXES, None),
            P(SEQ_AXES, FSDP_AXES, None),
        ),
        check_vma=False,
    )
```

```python
import jax
import jax.numpy as jnp
from jax import lax
from jax.experimental import pallas as pl
from jax.experimental.pallas import tpu as pltpu
from jax.sharding import PartitionSpec as P

QUERY_HEADS = 32
KEY_VALUE_HEADS = 4
HEAD_SIZE = 64
WINDOW = 128


rope_base = 150000.0


def from_behind(array, axis, by):
    peers = lax.axis_size(axis)
    pairs = [(i, i + by) for i in range(peers) if 0 <= i + by < peers]
    return lax.ppermute(array, axis, pairs)


def rope_tables(positions):
    half_width = HEAD_SIZE // 2
    frequency = rope_base ** (-jnp.arange(half_width, dtype=jnp.float32) / half_width)
    angle = positions.astype(jnp.float32)[:, None] * frequency[None, :]
    return (jnp.cos(angle), jnp.sin(angle))


def apply_rotary(values, cosine_lookup, sine_lookup, head_count, direction):
    row_count = values.shape[0]
    halves = values.reshape(row_count, head_count, 2, HEAD_SIZE // 2)
    front_half = halves[:, :, 0]
    back_half = halves[:, :, 1]
    cosine_rows = cosine_lookup[:, None, :]
    sine_rows = sine_lookup[:, None, :] * direction
    turned = jnp.stack(
        [
            front_half * cosine_rows - back_half * sine_rows,
            front_half * sine_rows + back_half * cosine_rows,
        ],
        axis=2,
    )
    return turned.reshape(row_count, head_count * HEAD_SIZE)


def band_kernel(sink_ref, lead_ref, q_ref, g_ref, k_ref, v_ref, attn_ref, dq_ref, dk_ref, dv_ref):
    score_scale = HEAD_SIZE ** (-0.5)
    group_width = QUERY_HEADS // KEY_VALUE_HEADS
    pair_width = 2 * HEAD_SIZE
    row_count = q_ref.shape[0]
    key_count = k_ref.shape[2]
    rows = lax.broadcasted_iota(jnp.int32, (row_count, key_count), 0)
    cols = lax.broadcasted_iota(jnp.int32, (row_count, key_count), 1)
    allowed = (cols > rows) & (cols <= rows + WINDOW) & (cols >= lead_ref[0])
    lanes = lax.broadcasted_iota(jnp.int32, (row_count, pair_width), 1)
    halves = (lanes < HEAD_SIZE, lanes >= HEAD_SIZE)
    trans_a = (((0,), (0,)), ((), ()))
    trans_b = (((1,), (1,)), ((), ()))
    for group in range(KEY_VALUE_HEADS):
        key_acc = jnp.zeros((key_count, pair_width), jnp.float32)
        value_acc = jnp.zeros((key_count, pair_width), jnp.float32)
        for pair in range(group_width // 2):
            col = (group * group_width + 2 * pair) * HEAD_SIZE
            query_p = q_ref[:, col : col + pair_width]
            grad_p = g_ref[:, col : col + pair_width]
            attn_acc = jnp.zeros((row_count, pair_width), jnp.float32)
            dq_acc = jnp.zeros((row_count, pair_width), jnp.float32)
            for side in range(2):
                head = group * group_width + 2 * pair + side
                key_s = k_ref[group, side]
                value_s = v_ref[group, side]
                scores = (
                    lax.dot_general(query_p, key_s, trans_b, preferred_element_type=jnp.float32)
                    * score_scale
                )
                exponent = jnp.where(allowed, jnp.exp(scores), 0.0)
                denominator = sink_ref[head] + jnp.sum(exponent, axis=1, keepdims=True)
                softmax_w = exponent * (1.0 / denominator)
                softmax_b = softmax_w.astype(jnp.bfloat16)
                attn_acc = attn_acc + jnp.dot(
                    softmax_b, value_s, preferred_element_type=jnp.float32
                )
                dprob = lax.dot_general(grad_p, value_s, trans_b, preferred_element_type=jnp.float32)
                row_delta = jnp.sum(softmax_w * dprob, axis=1, keepdims=True)
                dscore = (softmax_w * (dprob - row_delta) * score_scale).astype(jnp.bfloat16)
                dq_acc = dq_acc + jnp.dot(dscore, key_s, preferred_element_type=jnp.float32)
                query_h = jnp.where(halves[side], query_p, jnp.zeros_like(query_p))
                grad_h = jnp.where(halves[side], grad_p, jnp.zeros_like(grad_p))
                key_acc = key_acc + lax.dot_general(
                    dscore, query_h, trans_a, preferred_element_type=jnp.float32
                )
                value_acc = value_acc + lax.dot_general(
                    softmax_b, grad_h, trans_a, preferred_element_type=jnp.float32
                )
            attn_ref[:, col : col + pair_width] = attn_acc.astype(jnp.bfloat16)
            dq_ref[:, col : col + pair_width] = dq_acc
        dk_ref[group] = key_acc
        dv_ref[group] = value_acc


def padded_heads(columns, key_total):
    heads = columns.reshape(key_total, KEY_VALUE_HEADS, HEAD_SIZE).transpose(1, 0, 2)
    blank = jnp.zeros_like(heads)
    return jnp.stack(
        [jnp.concatenate([heads, blank], axis=2), jnp.concatenate([blank, heads], axis=2)], axis=1
    )


def band_attention(query_rot, keys_all, grad_out, sink_logit_values, row_start):
    row_total = query_rot.shape[0]
    key_total = keys_all.shape[0]
    key_span_width = KEY_VALUE_HEADS * HEAD_SIZE
    k_pairs = padded_heads(keys_all[:, :key_span_width], key_total)
    v_pairs = padded_heads(keys_all[:, key_span_width:], key_total)
    sink_weight = jnp.exp(sink_logit_values)
    lead = jnp.maximum(WINDOW - row_start, 0).astype(jnp.int32).reshape(1)
    smem = pl.BlockSpec(memory_space=pltpu.SMEM)
    vmem = pl.BlockSpec(memory_space=pltpu.VMEM)
    acc_shape = (KEY_VALUE_HEADS, key_total, 2 * HEAD_SIZE)
    attended, query_diff, dk_pairs, dv_pairs = pl.pallas_call(
        band_kernel,
        out_shape=(
            jax.ShapeDtypeStruct(query_rot.shape, jnp.bfloat16),
            jax.ShapeDtypeStruct(query_rot.shape, jnp.float32),
            jax.ShapeDtypeStruct(acc_shape, jnp.float32),
            jax.ShapeDtypeStruct(acc_shape, jnp.float32),
        ),
        in_specs=[smem, smem, vmem, vmem, vmem, vmem],
        out_specs=(vmem, vmem, vmem, vmem),
    )(sink_weight, lead, query_rot, grad_out, k_pairs, v_pairs)
    dk_h = dk_pairs[:, :, :HEAD_SIZE] + dk_pairs[:, :, HEAD_SIZE:]
    dv_h = dv_pairs[:, :, :HEAD_SIZE] + dv_pairs[:, :, HEAD_SIZE:]
    kv_diff = jnp.concatenate(
        [
            dk_h.transpose(1, 0, 2).reshape(key_total, key_span_width),
            dv_h.transpose(1, 0, 2).reshape(key_total, key_span_width),
        ],
        axis=1,
    )
    return attended, query_diff, kv_diff


FSDP_AXES = ("z", "xl", "c")
SEQ_AXES = ("xh", "y")


def gather_by_exchange(array, axes):
    peers = lax.axis_size(axes)
    copies = jnp.broadcast_to(array[None], (peers,) + array.shape)
    copies = lax.all_to_all(copies, axes, split_axis=0, concat_axis=0, tiled=True)
    return copies.reshape(peers * array.shape[0], *array.shape[1:])


def gather_pair(array, axis):
    other = lax.ppermute(array, axis, [(0, 1), (1, 0)])
    first = lax.axis_index(axis) == 0
    return jnp.concatenate(
        [jnp.where(first, array, other), jnp.where(first, other, array)], axis=0
    )


def local(tokens, queries, kv_weight, sink_logit_values, roll_offsets, out_grad):
    token_rows = tokens[0]
    query_rows = queries[0]
    grad_rows = out_grad[0]
    row_total = token_rows.shape[0]
    key_span_width = KEY_VALUE_HEADS * HEAD_SIZE
    seq_index = lax.axis_index(SEQ_AXES)
    seq_count = lax.axis_size(SEQ_AXES)
    stream_length = row_total * seq_count
    row_start = seq_index * row_total
    whole_weight = lax.all_gather(kv_weight, FSDP_AXES[1:], axis=0, tiled=True)
    whole_weight = lax.all_gather(whole_weight, FSDP_AXES[0], axis=0, tiled=True)
    feature_block = lax.all_to_all(token_rows, SEQ_AXES, split_axis=1, concat_axis=0, tiled=True)
    whole_weight, feature_block = lax.optimization_barrier((whole_weight, feature_block))
    projected_rows = jnp.dot(token_rows, whole_weight, preferred_element_type=jnp.float32)
    positions = (
        row_start + jnp.arange(row_total, dtype=jnp.int32) + roll_offsets[0]
    ) % stream_length
    cosine_lookup, sine_lookup = rope_tables(positions)
    key_value_rotated = jnp.concatenate(
        [
            apply_rotary(
                projected_rows[:, :key_span_width], cosine_lookup, sine_lookup, KEY_VALUE_HEADS, 1.0
            ),
            projected_rows[:, key_span_width:],
        ],
        axis=1,
    ).astype(jnp.bfloat16)
    query_rot = apply_rotary(
        query_rows.astype(jnp.float32), cosine_lookup, sine_lookup, QUERY_HEADS, 1.0
    ).astype(jnp.bfloat16)
    edge_rows = from_behind(key_value_rotated, SEQ_AXES, 1)
    keys_all = jnp.concatenate([edge_rows, key_value_rotated], axis=0)
    attended, query_diff, grad_all = band_attention(
        query_rot, keys_all, grad_rows, sink_logit_values, row_start
    )
    incoming = from_behind(grad_all[:WINDOW].astype(jnp.bfloat16), SEQ_AXES, -1).astype(
        jnp.float32
    )
    local_gradient = grad_all[WINDOW:]
    local_gradient = jnp.concatenate(
        [local_gradient[: row_total - WINDOW], local_gradient + incoming], axis=0
    )
    query_back = apply_rotary(query_diff, cosine_lookup, sine_lookup, QUERY_HEADS, -1.0).astype(
        jnp.bfloat16
    )
    key_value_backward = jnp.concatenate(
        [
            apply_rotary(
                local_gradient[:, :key_span_width],
                cosine_lookup,
                sine_lookup,
                KEY_VALUE_HEADS,
                -1.0,
            ),
            local_gradient[:, key_span_width:],
        ],
        axis=1,
    ).astype(jnp.bfloat16)
    token_back = lax.dot_general(
        key_value_backward,
        whole_weight,
        (((1,), (1,)), ((), ())),
        preferred_element_type=jnp.float32,
    ).astype(jnp.bfloat16)
    block_term = lax.dot_general(
        feature_block,
        gather_pair(gather_by_exchange(key_value_backward, SEQ_AXES[1:]), SEQ_AXES[0]),
        (((0,), (0,)), ((), ())),
        preferred_element_type=jnp.float32,
    )
    fsdp_count = lax.axis_size(FSDP_AXES)
    share = block_term.reshape(fsdp_count, -1, 128).astype(jnp.bfloat16)
    share = lax.all_to_all(share, FSDP_AXES, split_axis=0, concat_axis=0, tiled=True)
    weight_share = jnp.sum(share.astype(jnp.float32), axis=0)
    return (attended[None], query_back[None], token_back[None], weight_share[None])


def solution(mesh):
    fsdp_count = mesh.shape["fsdp"]
    seq_count = mesh.shape["seq"]
    split_mesh = jax.sharding.Mesh(
        mesh.devices.reshape(fsdp_count // 4, 2, 2, 2, seq_count // 2), FSDP_AXES + SEQ_AXES
    )
    placed = (
        P(FSDP_AXES, SEQ_AXES, None),
        P(FSDP_AXES, SEQ_AXES, None),
        P(FSDP_AXES, None),
        P(),
        P(FSDP_AXES),
        P(FSDP_AXES, SEQ_AXES, None),
    )
    return jax.shard_map(
        local,
        mesh=split_mesh,
        in_specs=placed,
        out_specs=(
            P(FSDP_AXES, SEQ_AXES, None),
            P(FSDP_AXES, SEQ_AXES, None),
            P(FSDP_AXES, SEQ_AXES, None),
            P(SEQ_AXES, FSDP_AXES, None),
        ),
        check_vma=False,
    )
```

```python
import jax
import jax.numpy as jnp
from jax import lax
from jax.experimental import pallas as pl
from jax.experimental.pallas import tpu as pltpu
from jax.sharding import PartitionSpec as P

QUERY_HEADS = 32
KEY_VALUE_HEADS = 4
HEAD_SIZE = 64
WINDOW = 128


rope_base = 150000.0


def from_behind(array, axis, by):
    peers = lax.axis_size(axis)
    pairs = [(i, i + by) for i in range(peers) if 0 <= i + by < peers]
    return lax.ppermute(array, axis, pairs)


def rope_tables(positions):
    half_width = HEAD_SIZE // 2
    frequency = rope_base ** (-jnp.arange(half_width, dtype=jnp.float32) / half_width)
    angle = positions.astype(jnp.float32)[:, None] * frequency[None, :]
    return (jnp.cos(angle), jnp.sin(angle))


def apply_rotary(values, cosine_lookup, sine_lookup, head_count, direction):
    row_count = values.shape[0]
    halves = values.reshape(row_count, head_count, 2, HEAD_SIZE // 2)
    front_half = halves[:, :, 0]
    back_half = halves[:, :, 1]
    cosine_rows = cosine_lookup[:, None, :]
    sine_rows = sine_lookup[:, None, :] * direction
    turned = jnp.stack(
        [
            front_half * cosine_rows - back_half * sine_rows,
            front_half * sine_rows + back_half * cosine_rows,
        ],
        axis=2,
    )
    return turned.reshape(row_count, head_count * HEAD_SIZE)


def band_kernel(sink_ref, lead_ref, q_ref, g_ref, k_ref, v_ref, attn_ref, dq_ref, dk_ref, dv_ref):
    score_scale = HEAD_SIZE ** (-0.5)
    group_width = QUERY_HEADS // KEY_VALUE_HEADS
    pair_width = 2 * HEAD_SIZE
    row_count = q_ref.shape[0]
    key_count = k_ref.shape[2]
    rows = lax.broadcasted_iota(jnp.int32, (row_count, key_count), 0)
    cols = lax.broadcasted_iota(jnp.int32, (row_count, key_count), 1)
    allowed = (cols > rows) & (cols <= rows + WINDOW) & (cols >= lead_ref[0])
    lanes = lax.broadcasted_iota(jnp.int32, (row_count, pair_width), 1)
    halves = (lanes < HEAD_SIZE, lanes >= HEAD_SIZE)
    trans_a = (((0,), (0,)), ((), ()))
    trans_b = (((1,), (1,)), ((), ()))
    for group in range(KEY_VALUE_HEADS):
        key_acc = jnp.zeros((key_count, pair_width), jnp.float32)
        value_acc = jnp.zeros((key_count, pair_width), jnp.float32)
        for pair in range(group_width // 2):
            col = (group * group_width + 2 * pair) * HEAD_SIZE
            query_p = q_ref[:, col : col + pair_width]
            grad_p = g_ref[:, col : col + pair_width]
            attn_acc = jnp.zeros((row_count, pair_width), jnp.float32)
            dq_acc = jnp.zeros((row_count, pair_width), jnp.float32)
            for side in range(2):
                head = group * group_width + 2 * pair + side
                key_s = k_ref[group, side]
                value_s = v_ref[group, side]
                scores = (
                    lax.dot_general(query_p, key_s, trans_b, preferred_element_type=jnp.float32)
                    * score_scale
                )
                exponent = jnp.where(allowed, jnp.exp(scores), 0.0)
                denominator = sink_ref[head] + jnp.sum(exponent, axis=1, keepdims=True)
                softmax_w = exponent * (1.0 / denominator)
                softmax_b = softmax_w.astype(jnp.bfloat16)
                attn_acc = attn_acc + jnp.dot(
                    softmax_b, value_s, preferred_element_type=jnp.float32
                )
                dprob = lax.dot_general(grad_p, value_s, trans_b, preferred_element_type=jnp.float32)
                row_delta = jnp.sum(softmax_w * dprob, axis=1, keepdims=True)
                dscore = (softmax_w * (dprob - row_delta) * score_scale).astype(jnp.bfloat16)
                dq_acc = dq_acc + jnp.dot(dscore, key_s, preferred_element_type=jnp.float32)
                query_h = jnp.where(halves[side], query_p, jnp.zeros_like(query_p))
                grad_h = jnp.where(halves[side], grad_p, jnp.zeros_like(grad_p))
                key_acc = key_acc + lax.dot_general(
                    dscore, query_h, trans_a, preferred_element_type=jnp.float32
                )
                value_acc = value_acc + lax.dot_general(
                    softmax_b, grad_h, trans_a, preferred_element_type=jnp.float32
                )
            attn_ref[:, col : col + pair_width] = attn_acc.astype(jnp.bfloat16)
            dq_ref[:, col : col + pair_width] = dq_acc
        dk_ref[group] = key_acc
        dv_ref[group] = value_acc


def padded_heads(columns, key_total):
    heads = columns.reshape(key_total, KEY_VALUE_HEADS, HEAD_SIZE).transpose(1, 0, 2)
    blank = jnp.zeros_like(heads)
    return jnp.stack(
        [jnp.concatenate([heads, blank], axis=2), jnp.concatenate([blank, heads], axis=2)], axis=1
    )


def band_attention(query_rot, keys_all, grad_out, sink_logit_values, row_start):
    row_total = query_rot.shape[0]
    key_total = keys_all.shape[0]
    key_span_width = KEY_VALUE_HEADS * HEAD_SIZE
    k_pairs = padded_heads(keys_all[:, :key_span_width], key_total)
    v_pairs = padded_heads(keys_all[:, key_span_width:], key_total)
    sink_weight = jnp.exp(sink_logit_values)
    lead = jnp.maximum(WINDOW - row_start, 0).astype(jnp.int32).reshape(1)
    smem = pl.BlockSpec(memory_space=pltpu.SMEM)
    vmem = pl.BlockSpec(memory_space=pltpu.VMEM)
    acc_shape = (KEY_VALUE_HEADS, key_total, 2 * HEAD_SIZE)
    attended, query_diff, dk_pairs, dv_pairs = pl.pallas_call(
        band_kernel,
        out_shape=(
            jax.ShapeDtypeStruct(query_rot.shape, jnp.bfloat16),
            jax.ShapeDtypeStruct(query_rot.shape, jnp.float32),
            jax.ShapeDtypeStruct(acc_shape, jnp.float32),
            jax.ShapeDtypeStruct(acc_shape, jnp.float32),
        ),
        in_specs=[smem, smem, vmem, vmem, vmem, vmem],
        out_specs=(vmem, vmem, vmem, vmem),
    )(sink_weight, lead, query_rot, grad_out, k_pairs, v_pairs)
    dk_h = dk_pairs[:, :, :HEAD_SIZE] + dk_pairs[:, :, HEAD_SIZE:]
    dv_h = dv_pairs[:, :, :HEAD_SIZE] + dv_pairs[:, :, HEAD_SIZE:]
    kv_diff = jnp.concatenate(
        [
            dk_h.transpose(1, 0, 2).reshape(key_total, key_span_width),
            dv_h.transpose(1, 0, 2).reshape(key_total, key_span_width),
        ],
        axis=1,
    )
    return attended, query_diff, kv_diff


FSDP_AXES = ("z", "xl", "c")
SEQ_AXES = ("xh", "y")


def gather_by_exchange(array, axes):
    peers = lax.axis_size(axes)
    copies = jnp.broadcast_to(array[None], (peers,) + array.shape)
    copies = lax.all_to_all(copies, axes, split_axis=0, concat_axis=0, tiled=True)
    return copies.reshape(peers * array.shape[0], *array.shape[1:])


def gather_pair(array, axis):
    other = lax.ppermute(array, axis, [(0, 1), (1, 0)])
    first = lax.axis_index(axis) == 0
    return jnp.concatenate(
        [jnp.where(first, array, other), jnp.where(first, other, array)], axis=0
    )


def local(tokens, queries, kv_weight, sink_logit_values, roll_offsets, out_grad):
    token_rows = tokens[0]
    query_rows = queries[0]
    grad_rows = out_grad[0]
    row_total = token_rows.shape[0]
    key_span_width = KEY_VALUE_HEADS * HEAD_SIZE
    seq_index = lax.axis_index(SEQ_AXES)
    seq_count = lax.axis_size(SEQ_AXES)
    stream_length = row_total * seq_count
    row_start = seq_index * row_total
    whole_weight = lax.all_gather(kv_weight, FSDP_AXES[1:], axis=0, tiled=True)
    whole_weight = lax.all_gather(whole_weight, FSDP_AXES[0], axis=0, tiled=True)
    feature_block = lax.all_to_all(token_rows, SEQ_AXES, split_axis=1, concat_axis=0, tiled=True)
    whole_weight, feature_block = lax.optimization_barrier((whole_weight, feature_block))
    projected_rows = jnp.dot(token_rows, whole_weight, preferred_element_type=jnp.float32)
    positions = (
        row_start + jnp.arange(row_total, dtype=jnp.int32) + roll_offsets[0]
    ) % stream_length
    cosine_lookup, sine_lookup = rope_tables(positions)
    key_value_rotated = jnp.concatenate(
        [
            apply_rotary(
                projected_rows[:, :key_span_width], cosine_lookup, sine_lookup, KEY_VALUE_HEADS, 1.0
            ),
            projected_rows[:, key_span_width:],
        ],
        axis=1,
    ).astype(jnp.bfloat16)
    query_rot = apply_rotary(
        query_rows.astype(jnp.float32), cosine_lookup, sine_lookup, QUERY_HEADS, 1.0
    ).astype(jnp.bfloat16)
    edge_rows = from_behind(key_value_rotated, SEQ_AXES, 1)
    keys_all = jnp.concatenate([edge_rows, key_value_rotated], axis=0)
    attended, query_diff, grad_all = band_attention(
        query_rot, keys_all, grad_rows, sink_logit_values, row_start
    )
    incoming = from_behind(grad_all[:WINDOW].astype(jnp.bfloat16), SEQ_AXES, -1).astype(
        jnp.float32
    )
    local_gradient = grad_all[WINDOW:]
    local_gradient = jnp.concatenate(
        [local_gradient[: row_total - WINDOW], local_gradient + incoming], axis=0
    )
    query_back = apply_rotary(query_diff, cosine_lookup, sine_lookup, QUERY_HEADS, -1.0).astype(
        jnp.bfloat16
    )
    key_value_backward = jnp.concatenate(
        [
            apply_rotary(
                local_gradient[:, :key_span_width],
                cosine_lookup,
                sine_lookup,
                KEY_VALUE_HEADS,
                -1.0,
            ),
            local_gradient[:, key_span_width:],
        ],
        axis=1,
    ).astype(jnp.bfloat16)
    token_back = lax.dot_general(
        key_value_backward,
        whole_weight,
        (((1,), (1,)), ((), ())),
        preferred_element_type=jnp.float32,
    ).astype(jnp.bfloat16)
    own_grads = gather_by_exchange(key_value_backward, SEQ_AXES[1:])
    other_grads = lax.ppermute(own_grads, SEQ_AXES[0], [(0, 1), (1, 0)])
    half_rows = own_grads.shape[0]
    first_half = lax.axis_index(SEQ_AXES[0]) == 0
    own_features = jnp.where(first_half, feature_block[:half_rows], feature_block[half_rows:])
    other_features = jnp.where(first_half, feature_block[half_rows:], feature_block[:half_rows])
    contract = (((0,), (0,)), ((), ()))
    block_term = lax.dot_general(
        own_features, own_grads, contract, preferred_element_type=jnp.float32
    ) + lax.dot_general(other_features, other_grads, contract, preferred_element_type=jnp.float32)
    fsdp_count = lax.axis_size(FSDP_AXES)
    share = block_term.reshape(fsdp_count, -1, 128).astype(jnp.bfloat16)
    share = lax.all_to_all(share, FSDP_AXES, split_axis=0, concat_axis=0, tiled=True)
    weight_share = jnp.sum(share.astype(jnp.float32), axis=0)
    return (attended[None], query_back[None], token_back[None], weight_share[None])


def solution(mesh):
    fsdp_count = mesh.shape["fsdp"]
    seq_count = mesh.shape["seq"]
    split_mesh = jax.sharding.Mesh(
        mesh.devices.reshape(fsdp_count // 4, 2, 2, 2, seq_count // 2), FSDP_AXES + SEQ_AXES
    )
    placed = (
        P(FSDP_AXES, SEQ_AXES, None),
        P(FSDP_AXES, SEQ_AXES, None),
        P(FSDP_AXES, None),
        P(),
        P(FSDP_AXES),
        P(FSDP_AXES, SEQ_AXES, None),
    )
    return jax.shard_map(
        local,
        mesh=split_mesh,
        in_specs=placed,
        out_specs=(
            P(FSDP_AXES, SEQ_AXES, None),
            P(FSDP_AXES, SEQ_AXES, None),
            P(FSDP_AXES, SEQ_AXES, None),
            P(SEQ_AXES, FSDP_AXES, None),
        ),
        check_vma=False,
    )
```

```python
import jax
import jax.numpy as jnp
from jax import lax
from jax.experimental import pallas as pl
from jax.experimental.pallas import tpu as pltpu
from jax.sharding import PartitionSpec as P

QUERY_HEADS = 32
KEY_VALUE_HEADS = 4
HEAD_SIZE = 64
WINDOW = 128


rope_base = 150000.0


def from_behind(array, axis, by):
    peers = lax.axis_size(axis)
    pairs = [(i, i + by) for i in range(peers) if 0 <= i + by < peers]
    return lax.ppermute(array, axis, pairs)


def rope_tables(positions):
    half_width = HEAD_SIZE // 2
    frequency = rope_base ** (-jnp.arange(half_width, dtype=jnp.float32) / half_width)
    angle = positions.astype(jnp.float32)[:, None] * frequency[None, :]
    return (jnp.cos(angle), jnp.sin(angle))


def apply_rotary(values, cosine_lookup, sine_lookup, head_count, direction):
    row_count = values.shape[0]
    halves = values.reshape(row_count, head_count, 2, HEAD_SIZE // 2)
    front_half = halves[:, :, 0]
    back_half = halves[:, :, 1]
    cosine_rows = cosine_lookup[:, None, :]
    sine_rows = sine_lookup[:, None, :] * direction
    turned = jnp.stack(
        [
            front_half * cosine_rows - back_half * sine_rows,
            front_half * sine_rows + back_half * cosine_rows,
        ],
        axis=2,
    )
    return turned.reshape(row_count, head_count * HEAD_SIZE)


def band_kernel(sink_ref, lead_ref, q_ref, g_ref, k_ref, v_ref, attn_ref, dq_ref, dk_ref, dv_ref):
    score_scale = HEAD_SIZE ** (-0.5)
    group_width = QUERY_HEADS // KEY_VALUE_HEADS
    pair_width = 2 * HEAD_SIZE
    row_count = q_ref.shape[0]
    key_count = k_ref.shape[2]
    rows = lax.broadcasted_iota(jnp.int32, (row_count, key_count), 0)
    cols = lax.broadcasted_iota(jnp.int32, (row_count, key_count), 1)
    allowed = (cols > rows) & (cols <= rows + WINDOW) & (cols >= lead_ref[0])
    lanes = lax.broadcasted_iota(jnp.int32, (row_count, pair_width), 1)
    halves = (lanes < HEAD_SIZE, lanes >= HEAD_SIZE)
    trans_a = (((0,), (0,)), ((), ()))
    trans_b = (((1,), (1,)), ((), ()))
    for group in range(KEY_VALUE_HEADS):
        key_acc = jnp.zeros((key_count, pair_width), jnp.float32)
        value_acc = jnp.zeros((key_count, pair_width), jnp.float32)
        for pair in range(group_width // 2):
            col = (group * group_width + 2 * pair) * HEAD_SIZE
            query_p = q_ref[:, col : col + pair_width]
            grad_p = g_ref[:, col : col + pair_width]
            attn_acc = jnp.zeros((row_count, pair_width), jnp.float32)
            dq_acc = jnp.zeros((row_count, pair_width), jnp.float32)
            score_parts, prob_parts, query_parts, grad_parts = [], [], [], []
            for side in range(2):
                head = group * group_width + 2 * pair + side
                key_s = k_ref[group, side]
                value_s = v_ref[group, side]
                scores = (
                    lax.dot_general(query_p, key_s, trans_b, preferred_element_type=jnp.float32)
                    * score_scale
                )
                exponent = jnp.where(allowed, jnp.exp(scores), 0.0)
                denominator = sink_ref[head] + jnp.sum(exponent, axis=1, keepdims=True)
                softmax_w = exponent * (1.0 / denominator)
                softmax_b = softmax_w.astype(jnp.bfloat16)
                attn_acc = attn_acc + jnp.dot(
                    softmax_b, value_s, preferred_element_type=jnp.float32
                )
                dprob = lax.dot_general(grad_p, value_s, trans_b, preferred_element_type=jnp.float32)
                row_delta = jnp.sum(softmax_w * dprob, axis=1, keepdims=True)
                dscore = (softmax_w * (dprob - row_delta) * score_scale).astype(jnp.bfloat16)
                dq_acc = dq_acc + jnp.dot(dscore, key_s, preferred_element_type=jnp.float32)
                score_parts.append(dscore)
                prob_parts.append(softmax_b)
                query_parts.append(jnp.where(halves[side], query_p, jnp.zeros_like(query_p)))
                grad_parts.append(jnp.where(halves[side], grad_p, jnp.zeros_like(grad_p)))
            key_acc = key_acc + lax.dot_general(
                jnp.concatenate(score_parts, axis=0),
                jnp.concatenate(query_parts, axis=0),
                trans_a,
                preferred_element_type=jnp.float32,
            )
            value_acc = value_acc + lax.dot_general(
                jnp.concatenate(prob_parts, axis=0),
                jnp.concatenate(grad_parts, axis=0),
                trans_a,
                preferred_element_type=jnp.float32,
            )
            attn_ref[:, col : col + pair_width] = attn_acc.astype(jnp.bfloat16)
            dq_ref[:, col : col + pair_width] = dq_acc
        dk_ref[group] = key_acc
        dv_ref[group] = value_acc


def padded_heads(columns, key_total):
    heads = columns.reshape(key_total, KEY_VALUE_HEADS, HEAD_SIZE).transpose(1, 0, 2)
    blank = jnp.zeros_like(heads)
    return jnp.stack(
        [jnp.concatenate([heads, blank], axis=2), jnp.concatenate([blank, heads], axis=2)], axis=1
    )


def band_attention(query_rot, keys_all, grad_out, sink_logit_values, row_start):
    row_total = query_rot.shape[0]
    key_total = keys_all.shape[0]
    key_span_width = KEY_VALUE_HEADS * HEAD_SIZE
    k_pairs = padded_heads(keys_all[:, :key_span_width], key_total)
    v_pairs = padded_heads(keys_all[:, key_span_width:], key_total)
    sink_weight = jnp.exp(sink_logit_values)
    lead = jnp.maximum(WINDOW - row_start, 0).astype(jnp.int32).reshape(1)
    smem = pl.BlockSpec(memory_space=pltpu.SMEM)
    vmem = pl.BlockSpec(memory_space=pltpu.VMEM)
    acc_shape = (KEY_VALUE_HEADS, key_total, 2 * HEAD_SIZE)
    attended, query_diff, dk_pairs, dv_pairs = pl.pallas_call(
        band_kernel,
        out_shape=(
            jax.ShapeDtypeStruct(query_rot.shape, jnp.bfloat16),
            jax.ShapeDtypeStruct(query_rot.shape, jnp.float32),
            jax.ShapeDtypeStruct(acc_shape, jnp.float32),
            jax.ShapeDtypeStruct(acc_shape, jnp.float32),
        ),
        in_specs=[smem, smem, vmem, vmem, vmem, vmem],
        out_specs=(vmem, vmem, vmem, vmem),
    )(sink_weight, lead, query_rot, grad_out, k_pairs, v_pairs)
    dk_h = dk_pairs[:, :, :HEAD_SIZE] + dk_pairs[:, :, HEAD_SIZE:]
    dv_h = dv_pairs[:, :, :HEAD_SIZE] + dv_pairs[:, :, HEAD_SIZE:]
    kv_diff = jnp.concatenate(
        [
            dk_h.transpose(1, 0, 2).reshape(key_total, key_span_width),
            dv_h.transpose(1, 0, 2).reshape(key_total, key_span_width),
        ],
        axis=1,
    )
    return attended, query_diff, kv_diff


FSDP_AXES = ("z", "xl", "c")
SEQ_AXES = ("xh", "y")


def gather_by_exchange(array, axes):
    peers = lax.axis_size(axes)
    copies = jnp.broadcast_to(array[None], (peers,) + array.shape)
    copies = lax.all_to_all(copies, axes, split_axis=0, concat_axis=0, tiled=True)
    return copies.reshape(peers * array.shape[0], *array.shape[1:])


def gather_pair(array, axis):
    other = lax.ppermute(array, axis, [(0, 1), (1, 0)])
    first = lax.axis_index(axis) == 0
    return jnp.concatenate(
        [jnp.where(first, array, other), jnp.where(first, other, array)], axis=0
    )


def local(tokens, queries, kv_weight, sink_logit_values, roll_offsets, out_grad):
    token_rows = tokens[0]
    query_rows = queries[0]
    grad_rows = out_grad[0]
    row_total = token_rows.shape[0]
    key_span_width = KEY_VALUE_HEADS * HEAD_SIZE
    seq_index = lax.axis_index(SEQ_AXES)
    seq_count = lax.axis_size(SEQ_AXES)
    stream_length = row_total * seq_count
    row_start = seq_index * row_total
    whole_weight = lax.all_gather(kv_weight, FSDP_AXES[1:], axis=0, tiled=True)
    whole_weight = lax.all_gather(whole_weight, FSDP_AXES[0], axis=0, tiled=True)
    feature_block = lax.all_to_all(token_rows, SEQ_AXES, split_axis=1, concat_axis=0, tiled=True)
    whole_weight, feature_block = lax.optimization_barrier((whole_weight, feature_block))
    projected_rows = jnp.dot(token_rows, whole_weight, preferred_element_type=jnp.float32)
    positions = (
        row_start + jnp.arange(row_total, dtype=jnp.int32) + roll_offsets[0]
    ) % stream_length
    cosine_lookup, sine_lookup = rope_tables(positions)
    key_value_rotated = jnp.concatenate(
        [
            apply_rotary(
                projected_rows[:, :key_span_width], cosine_lookup, sine_lookup, KEY_VALUE_HEADS, 1.0
            ),
            projected_rows[:, key_span_width:],
        ],
        axis=1,
    ).astype(jnp.bfloat16)
    query_rot = apply_rotary(
        query_rows.astype(jnp.float32), cosine_lookup, sine_lookup, QUERY_HEADS, 1.0
    ).astype(jnp.bfloat16)
    edge_rows = from_behind(key_value_rotated, SEQ_AXES, 1)
    keys_all = jnp.concatenate([edge_rows, key_value_rotated], axis=0)
    attended, query_diff, grad_all = band_attention(
        query_rot, keys_all, grad_rows, sink_logit_values, row_start
    )
    incoming = from_behind(grad_all[:WINDOW].astype(jnp.bfloat16), SEQ_AXES, -1).astype(
        jnp.float32
    )
    local_gradient = grad_all[WINDOW:]
    local_gradient = jnp.concatenate(
        [local_gradient[: row_total - WINDOW], local_gradient + incoming], axis=0
    )
    query_back = apply_rotary(query_diff, cosine_lookup, sine_lookup, QUERY_HEADS, -1.0).astype(
        jnp.bfloat16
    )
    key_value_backward = jnp.concatenate(
        [
            apply_rotary(
                local_gradient[:, :key_span_width],
                cosine_lookup,
                sine_lookup,
                KEY_VALUE_HEADS,
                -1.0,
            ),
            local_gradient[:, key_span_width:],
        ],
        axis=1,
    ).astype(jnp.bfloat16)
    token_back = lax.dot_general(
        key_value_backward,
        whole_weight,
        (((1,), (1,)), ((), ())),
        preferred_element_type=jnp.float32,
    ).astype(jnp.bfloat16)
    block_term = lax.dot_general(
        feature_block,
        gather_pair(gather_by_exchange(key_value_backward, SEQ_AXES[1:]), SEQ_AXES[0]),
        (((0,), (0,)), ((), ())),
        preferred_element_type=jnp.float32,
    )
    fsdp_count = lax.axis_size(FSDP_AXES)
    share = block_term.reshape(fsdp_count, -1, 128).astype(jnp.bfloat16)
    share = lax.all_to_all(share, FSDP_AXES, split_axis=0, concat_axis=0, tiled=True)
    weight_share = jnp.sum(share.astype(jnp.float32), axis=0)
    return (attended[None], query_back[None], token_back[None], weight_share[None])


def solution(mesh):
    fsdp_count = mesh.shape["fsdp"]
    seq_count = mesh.shape["seq"]
    split_mesh = jax.sharding.Mesh(
        mesh.devices.reshape(fsdp_count // 4, 2, 2, 2, seq_count // 2), FSDP_AXES + SEQ_AXES
    )
    placed = (
        P(FSDP_AXES, SEQ_AXES, None),
        P(FSDP_AXES, SEQ_AXES, None),
        P(FSDP_AXES, None),
        P(),
        P(FSDP_AXES),
        P(FSDP_AXES, SEQ_AXES, None),
    )
    return jax.shard_map(
        local,
        mesh=split_mesh,
        in_specs=placed,
        out_specs=(
            P(FSDP_AXES, SEQ_AXES, None),
            P(FSDP_AXES, SEQ_AXES, None),
            P(FSDP_AXES, SEQ_AXES, None),
            P(SEQ_AXES, FSDP_AXES, None),
        ),
        check_vma=False,
    )
```

```python
import jax
import jax.numpy as jnp
from jax import lax
from jax.experimental import pallas as pl
from jax.experimental.pallas import tpu as pltpu
from jax.sharding import PartitionSpec as P

QUERY_HEADS = 32
KEY_VALUE_HEADS = 4
HEAD_SIZE = 64
WINDOW = 128


rope_base = 150000.0


def from_behind(array, axis, by):
    peers = lax.axis_size(axis)
    pairs = [(i, i + by) for i in range(peers) if 0 <= i + by < peers]
    return lax.ppermute(array, axis, pairs)


def rope_tables(positions):
    half_width = HEAD_SIZE // 2
    frequency = rope_base ** (-jnp.arange(half_width, dtype=jnp.float32) / half_width)
    angle = positions.astype(jnp.float32)[:, None] * frequency[None, :]
    return (jnp.cos(angle), jnp.sin(angle))


def apply_rotary(values, cosine_lookup, sine_lookup, head_count, direction):
    row_count = values.shape[0]
    halves = values.reshape(row_count, head_count, 2, HEAD_SIZE // 2)
    front_half = halves[:, :, 0]
    back_half = halves[:, :, 1]
    cosine_rows = cosine_lookup[:, None, :]
    sine_rows = sine_lookup[:, None, :] * direction
    turned = jnp.stack(
        [
            front_half * cosine_rows - back_half * sine_rows,
            front_half * sine_rows + back_half * cosine_rows,
        ],
        axis=2,
    )
    return turned.reshape(row_count, head_count * HEAD_SIZE)


def band_kernel(sink_ref, lead_ref, q_ref, g_ref, k_ref, v_ref, attn_ref, dq_ref, dk_ref, dv_ref):
    score_scale = HEAD_SIZE ** (-0.5)
    group_width = QUERY_HEADS // KEY_VALUE_HEADS
    pair_width = 2 * HEAD_SIZE
    row_count = q_ref.shape[0]
    key_count = k_ref.shape[2]
    rows = lax.broadcasted_iota(jnp.int32, (row_count, key_count), 0)
    cols = lax.broadcasted_iota(jnp.int32, (row_count, key_count), 1)
    allowed = (cols > rows) & (cols <= rows + WINDOW) & (cols >= lead_ref[0])
    lanes = lax.broadcasted_iota(jnp.int32, (row_count, pair_width), 1)
    halves = (lanes < HEAD_SIZE, lanes >= HEAD_SIZE)
    trans_a = (((0,), (0,)), ((), ()))
    trans_b = (((1,), (1,)), ((), ()))
    for group in range(KEY_VALUE_HEADS):
        key_acc = jnp.zeros((key_count, pair_width), jnp.float32)
        value_acc = jnp.zeros((key_count, pair_width), jnp.float32)
        for pair in range(group_width // 2):
            col = (group * group_width + 2 * pair) * HEAD_SIZE
            query_p = q_ref[:, col : col + pair_width]
            grad_p = g_ref[:, col : col + pair_width]
            attn_acc = jnp.zeros((row_count, pair_width), jnp.float32)
            dq_acc = jnp.zeros((row_count, pair_width), jnp.float32)
            score_parts, prob_parts, query_parts, grad_parts = [], [], [], []
            for side in range(2):
                head = group * group_width + 2 * pair + side
                key_s = k_ref[group, side]
                value_s = v_ref[group, side]
                scores = (
                    lax.dot_general(query_p, key_s, trans_b, preferred_element_type=jnp.float32)
                    * score_scale
                )
                exponent = jnp.where(allowed, jnp.exp(scores), 0.0)
                denominator = sink_ref[head] + jnp.sum(exponent, axis=1, keepdims=True)
                softmax_w = exponent * (1.0 / denominator)
                softmax_b = softmax_w.astype(jnp.bfloat16)
                dprob = lax.dot_general(grad_p, value_s, trans_b, preferred_element_type=jnp.float32)
                row_delta = jnp.sum(softmax_w * dprob, axis=1, keepdims=True)
                dscore = (softmax_w * (dprob - row_delta) * score_scale).astype(jnp.bfloat16)
                score_parts.append(dscore)
                prob_parts.append(softmax_b)
                query_parts.append(jnp.where(halves[side], query_p, jnp.zeros_like(query_p)))
                grad_parts.append(jnp.where(halves[side], grad_p, jnp.zeros_like(grad_p)))
            attn_acc = jnp.dot(
                jnp.concatenate(prob_parts, axis=1),
                jnp.concatenate([v_ref[group, 0], v_ref[group, 1]], axis=0),
                preferred_element_type=jnp.float32,
            )
            dq_acc = jnp.dot(
                jnp.concatenate(score_parts, axis=1),
                jnp.concatenate([k_ref[group, 0], k_ref[group, 1]], axis=0),
                preferred_element_type=jnp.float32,
            )
            key_acc = key_acc + lax.dot_general(
                jnp.concatenate(score_parts, axis=0),
                jnp.concatenate(query_parts, axis=0),
                trans_a,
                preferred_element_type=jnp.float32,
            )
            value_acc = value_acc + lax.dot_general(
                jnp.concatenate(prob_parts, axis=0),
                jnp.concatenate(grad_parts, axis=0),
                trans_a,
                preferred_element_type=jnp.float32,
            )
            attn_ref[:, col : col + pair_width] = attn_acc.astype(jnp.bfloat16)
            dq_ref[:, col : col + pair_width] = dq_acc
        dk_ref[group] = key_acc
        dv_ref[group] = value_acc


def padded_heads(columns, key_total):
    heads = columns.reshape(key_total, KEY_VALUE_HEADS, HEAD_SIZE).transpose(1, 0, 2)
    blank = jnp.zeros_like(heads)
    return jnp.stack(
        [jnp.concatenate([heads, blank], axis=2), jnp.concatenate([blank, heads], axis=2)], axis=1
    )


def band_attention(query_rot, keys_all, grad_out, sink_logit_values, row_start):
    row_total = query_rot.shape[0]
    key_total = keys_all.shape[0]
    key_span_width = KEY_VALUE_HEADS * HEAD_SIZE
    k_pairs = padded_heads(keys_all[:, :key_span_width], key_total)
    v_pairs = padded_heads(keys_all[:, key_span_width:], key_total)
    sink_weight = jnp.exp(sink_logit_values)
    lead = jnp.maximum(WINDOW - row_start, 0).astype(jnp.int32).reshape(1)
    smem = pl.BlockSpec(memory_space=pltpu.SMEM)
    vmem = pl.BlockSpec(memory_space=pltpu.VMEM)
    acc_shape = (KEY_VALUE_HEADS, key_total, 2 * HEAD_SIZE)
    attended, query_diff, dk_pairs, dv_pairs = pl.pallas_call(
        band_kernel,
        out_shape=(
            jax.ShapeDtypeStruct(query_rot.shape, jnp.bfloat16),
            jax.ShapeDtypeStruct(query_rot.shape, jnp.float32),
            jax.ShapeDtypeStruct(acc_shape, jnp.float32),
            jax.ShapeDtypeStruct(acc_shape, jnp.float32),
        ),
        in_specs=[smem, smem, vmem, vmem, vmem, vmem],
        out_specs=(vmem, vmem, vmem, vmem),
    )(sink_weight, lead, query_rot, grad_out, k_pairs, v_pairs)
    dk_h = dk_pairs[:, :, :HEAD_SIZE] + dk_pairs[:, :, HEAD_SIZE:]
    dv_h = dv_pairs[:, :, :HEAD_SIZE] + dv_pairs[:, :, HEAD_SIZE:]
    kv_diff = jnp.concatenate(
        [
            dk_h.transpose(1, 0, 2).reshape(key_total, key_span_width),
            dv_h.transpose(1, 0, 2).reshape(key_total, key_span_width),
        ],
        axis=1,
    )
    return attended, query_diff, kv_diff


FSDP_AXES = ("z", "xl", "c")
SEQ_AXES = ("xh", "y")


def gather_by_exchange(array, axes):
    peers = lax.axis_size(axes)
    copies = jnp.broadcast_to(array[None], (peers,) + array.shape)
    copies = lax.all_to_all(copies, axes, split_axis=0, concat_axis=0, tiled=True)
    return copies.reshape(peers * array.shape[0], *array.shape[1:])


def gather_pair(array, axis):
    other = lax.ppermute(array, axis, [(0, 1), (1, 0)])
    first = lax.axis_index(axis) == 0
    return jnp.concatenate(
        [jnp.where(first, array, other), jnp.where(first, other, array)], axis=0
    )


def local(tokens, queries, kv_weight, sink_logit_values, roll_offsets, out_grad):
    token_rows = tokens[0]
    query_rows = queries[0]
    grad_rows = out_grad[0]
    row_total = token_rows.shape[0]
    key_span_width = KEY_VALUE_HEADS * HEAD_SIZE
    seq_index = lax.axis_index(SEQ_AXES)
    seq_count = lax.axis_size(SEQ_AXES)
    stream_length = row_total * seq_count
    row_start = seq_index * row_total
    whole_weight = lax.all_gather(kv_weight, FSDP_AXES[1:], axis=0, tiled=True)
    whole_weight = lax.all_gather(whole_weight, FSDP_AXES[0], axis=0, tiled=True)
    feature_block = lax.all_to_all(token_rows, SEQ_AXES, split_axis=1, concat_axis=0, tiled=True)
    whole_weight, feature_block = lax.optimization_barrier((whole_weight, feature_block))
    projected_rows = jnp.dot(token_rows, whole_weight, preferred_element_type=jnp.float32)
    positions = (
        row_start + jnp.arange(row_total, dtype=jnp.int32) + roll_offsets[0]
    ) % stream_length
    cosine_lookup, sine_lookup = rope_tables(positions)
    key_value_rotated = jnp.concatenate(
        [
            apply_rotary(
                projected_rows[:, :key_span_width], cosine_lookup, sine_lookup, KEY_VALUE_HEADS, 1.0
            ),
            projected_rows[:, key_span_width:],
        ],
        axis=1,
    ).astype(jnp.bfloat16)
    query_rot = apply_rotary(
        query_rows.astype(jnp.float32), cosine_lookup, sine_lookup, QUERY_HEADS, 1.0
    ).astype(jnp.bfloat16)
    edge_rows = from_behind(key_value_rotated, SEQ_AXES, 1)
    keys_all = jnp.concatenate([edge_rows, key_value_rotated], axis=0)
    attended, query_diff, grad_all = band_attention(
        query_rot, keys_all, grad_rows, sink_logit_values, row_start
    )
    incoming = from_behind(grad_all[:WINDOW].astype(jnp.bfloat16), SEQ_AXES, -1).astype(
        jnp.float32
    )
    local_gradient = grad_all[WINDOW:]
    local_gradient = jnp.concatenate(
        [local_gradient[: row_total - WINDOW], local_gradient + incoming], axis=0
    )
    query_back = apply_rotary(query_diff, cosine_lookup, sine_lookup, QUERY_HEADS, -1.0).astype(
        jnp.bfloat16
    )
    key_value_backward = jnp.concatenate(
        [
            apply_rotary(
                local_gradient[:, :key_span_width],
                cosine_lookup,
                sine_lookup,
                KEY_VALUE_HEADS,
                -1.0,
            ),
            local_gradient[:, key_span_width:],
        ],
        axis=1,
    ).astype(jnp.bfloat16)
    token_back = lax.dot_general(
        key_value_backward,
        whole_weight,
        (((1,), (1,)), ((), ())),
        preferred_element_type=jnp.float32,
    ).astype(jnp.bfloat16)
    block_term = lax.dot_general(
        feature_block,
        gather_pair(gather_by_exchange(key_value_backward, SEQ_AXES[1:]), SEQ_AXES[0]),
        (((0,), (0,)), ((), ())),
        preferred_element_type=jnp.float32,
    )
    fsdp_count = lax.axis_size(FSDP_AXES)
    share = block_term.reshape(fsdp_count, -1, 128).astype(jnp.bfloat16)
    share = lax.all_to_all(share, FSDP_AXES, split_axis=0, concat_axis=0, tiled=True)
    weight_share = jnp.sum(share.astype(jnp.float32), axis=0)
    return (attended[None], query_back[None], token_back[None], weight_share[None])


def solution(mesh):
    fsdp_count = mesh.shape["fsdp"]
    seq_count = mesh.shape["seq"]
    split_mesh = jax.sharding.Mesh(
        mesh.devices.reshape(fsdp_count // 4, 2, 2, 2, seq_count // 2), FSDP_AXES + SEQ_AXES
    )
    placed = (
        P(FSDP_AXES, SEQ_AXES, None),
        P(FSDP_AXES, SEQ_AXES, None),
        P(FSDP_AXES, None),
        P(),
        P(FSDP_AXES),
        P(FSDP_AXES, SEQ_AXES, None),
    )
    return jax.shard_map(
        local,
        mesh=split_mesh,
        in_specs=placed,
        out_specs=(
            P(FSDP_AXES, SEQ_AXES, None),
            P(FSDP_AXES, SEQ_AXES, None),
            P(FSDP_AXES, SEQ_AXES, None),
            P(SEQ_AXES, FSDP_AXES, None),
        ),
        check_vma=False,
    )
```
